32 devices in a mesh: rep: 2 (over x), member: 4 (over y, core), tp: 4 (over z).
Axes of the slice: x: 2, y: 2, z: 4, core: 2. Of those that a mesh axis runs over, the one named last changes fastest.
Arguments:
- states: bfloat16 [4096, 1024], P(('rep', 'member', 'tp')), parts along dimension 0, may hold values from -6 to 6
- member_of: int32 [4096, 1], P(('rep', 'member', 'tp')), parts along dimension 0, may hold values from 0 to 1; in each aligned block of 128 rows (0 to 127, 128 to 255, ...) at most 128 rows name the same one
- place: int32 [4096], P(('rep', 'member', 'tp')), parts along dimension 0, may hold values from 0 to 2047, as said below
- norm_gain: float32 [2, 1024], replicated, may hold values from 0.5 to 2
- w_up: bfloat16 [4, 1024, 2048], P('member', None, 'tp'), may hold values from -0.1875 to 0.1875
- w_down: bfloat16 [4, 2048, 1024], P('member', 'tp'), may hold values from -0.09375 to 0.09375
- policy_gain: float32 [1024], replicated, may hold values from 0.5 to 2
- w_policy: bfloat16 [1024, 128], replicated, may hold values from -0.1875 to 0.1875
Outputs:
- imagined: bfloat16 [4096, 1024], P(('rep', 'member', 'tp')), parts along dimension 0
- action: bfloat16 [4096, 128], P(('rep', 'member', 'tp')), parts along dimension 0
The draws below stay inside these ranges and needn't reach their ends.
There are 2 independent parts, one for each index of `rep`. The reference program is written for one: setup_inputs(seed, part) draws one part's arguments, and reference() takes and returns one part's arrays. A program takes and returns all parts, laid end to end along the dimension named above; an argument that names none is the same for every part. Nothing has to cross between parts.
Inputs may be any that keep to these rules, and one draw needn't show every extreme that they name: `member_of`: at most 128 of the rows of one device name any one member, and that count is reached on some device. `place`: A permutation of the 2048 learner positions; learner device k holds positions k * 128 to (k + 1) * 128 - 1, and the rows of each device go exactly 8 to every learner device.
All inputs are finite; a program needn't handle non-finite values.
Results may differ from the reference program's by a relative error of at most 0.0069.
Values may be sent and summed in bfloat16 or wider, within the bound.
No kernel may reach another device: no remote copies, remote signals or barrier semaphores. Data moves between devices by JAX's collectives and lax.ppermute only.
A program may use at most 128 MiB of HBM per device.

```python
import math
import jax
import jax.numpy as jnp
import numpy as np
from jax import lax

D = 1024
FF = 4096
ACT = 128
ROW_DEV = 128
MEMBERS = 2
ROWS = 2048
CAPM = 128
REGROUP = 8


def draw_place(key, part):
    sources = ROWS // ROW_DEV
    first_key, second_key = jax.random.split(key)

    def shuffled(inner_key):
        return jax.random.permutation(inner_key, ROW_DEV)
    spread = jax.vmap(shuffled)(jax.random.split(first_key, sources)).astype(jnp.int32)
    learner = spread // REGROUP
    within = spread % REGROUP
    sectioned = jnp.arange(sources, dtype=jnp.int32)[:, None] * REGROUP + within
    shuffle = jax.vmap(shuffled)(jax.random.split(second_key, sources)).astype(jnp.int32)
    final = shuffle[learner, sectioned]
    return (learner * ROW_DEV + final).reshape(-1).astype(jnp.int32)


def block_scale(stream_key, shape, cuts, low, high):
    loudness = 1.0
    for position, shards_of in cuts:
        steps = jax.random.uniform(jax.random.fold_in(jax.random.fold_in(stream_key, 6), position), (shards_of,), jnp.float32, low / len(cuts), high / len(cuts))
        loudness = loudness * jnp.repeat(jnp.exp(steps), shape[position] // shards_of).reshape((-1,) + (1,) * (len(shape) - 1 - position))
    return loudness


def routed_block(rng, own, number, rows, count, top, bound, skew):
    ranking = jax.random.permutation(rng, count)
    packed, ordinary = portions_of(count, rows * top, bound, skew, True), portions_of(count, rows * top, bound, skew, False)
    places = jnp.arange(count)

    def named(sizes, turn):
        used = int((sizes > 0).sum())
        fixed = max(1, used // 4)
        passed = fixed + (places - fixed + turn * (used - fixed)) % max(1, count - fixed)
        return jnp.zeros((count,), jnp.int32).at[ranking[jnp.where(places < fixed, places, passed)]].set(jnp.asarray(sizes, jnp.int32))

    sizes = jnp.where(number % 4 == 0, named(packed, number // 4), named(ordinary, number - number // 4 - 1))
    mixed = jax.random.permutation(jax.random.fold_in(own, 3), count)
    giver, sink = mixed[0:count // 2 * 2:2], mixed[1:count // 2 * 2:2]
    room = jnp.minimum(sizes[giver] - 1, bound - sizes[sink]) // 2
    room = jnp.where((giver == ranking[0]) | (sink == ranking[0]) | (sizes[sink] == 0), 0, jnp.maximum(room, 0))
    passed = jax.random.randint(jax.random.fold_in(own, 4), (count // 2,), 0, 1 << 20) % (room + 1)
    sizes = sizes.at[giver].add(-passed).at[sink].add(passed)
    labels = jnp.searchsorted(jnp.cumsum(sizes), jnp.arange(rows * top), side="right").astype(jnp.int32)
    table = labels.reshape(top, rows).T
    table = table[jax.random.permutation(jax.random.fold_in(own, 1), rows)]
    turn = jax.random.randint(jax.random.fold_in(own, 2), (rows, 1), 0, top)
    return jnp.take_along_axis(table, (jnp.arange(top)[None, :] + turn) % top, axis=1)


def portions_of(number_of, total, bound, skew, full):
    loads = [(1 << 20) // math.isqrt(rank ** skew) + 1 for rank in range(1, number_of + 1)]
    largest = bound if full else min(bound, max(-(-total // number_of), total * loads[0] // sum(loads)))
    least = 1 if total - largest >= number_of - 1 else 0
    holding, surplus = [largest] + [least] * (number_of - 1), total - largest - least * (number_of - 1)
    while surplus > 0:
        candidates = [i for i in range(1, number_of) if holding[i] < largest] or [i for i in range(1, number_of) if holding[i] < bound]
        pool, remaining = sum([loads[i] for i in candidates]), surplus
        for i in candidates:
            addition = min(bound - holding[i], max(1, remaining * loads[i] // pool), surplus)
            holding[i] = holding[i] + addition
            surplus = surplus - addition
    return np.array(holding)


def normal_values(rng, extent, deviation, reach, cuts=(), held_as=jnp.bfloat16):
    array = deviation * jax.random.normal(rng, extent, jnp.float32)
    if cuts:
        array = array * block_scale(rng, extent, cuts, -0.22, 0.18)
    return jnp.clip(array, -reach, reach).astype(held_as)


def setup_inputs(seed: int = 0, part: int = 0) -> dict:
    arg_keys = jax.random.split(jax.random.key(seed), 9)
    part_splits = jax.random.split(jax.random.fold_in(arg_keys[8], part), 9)
    states = normal_values(part_splits[0], (ROWS, D), 1.0, 6.0, ((0, 16),))
    member_of_keys = jax.random.split(jax.random.fold_in(part_splits[1], 1), ROWS // ROW_DEV)
    member_of_turns = jax.random.permutation(jax.random.fold_in(part_splits[1], 3), ROWS // ROW_DEV)
    member_of = jax.vmap(lambda own, number: routed_block(jax.random.fold_in(part_splits[1], 2), own, number, ROW_DEV, MEMBERS, 1, CAPM, 2))(member_of_keys, member_of_turns).reshape((ROWS, 1))
    place = draw_place(jax.random.fold_in(jax.random.fold_in(arg_keys[8], part), 71), part)
    norm_gain = jnp.clip(jnp.exp(jax.random.uniform(arg_keys[3], (MEMBERS, D), jnp.float32, math.log(0.5), math.log(2.0))), 0.5, 2.0)
    w_up = normal_values(arg_keys[4], (2 * MEMBERS, D, FF // 2), D ** -0.5, 0.1875, ((0, 4), (2, 4)))
    w_down = normal_values(arg_keys[5], (2 * MEMBERS, FF // 2, D), FF ** -0.5, 0.09375, ((0, 4), (1, 4)))
    policy_gain = jnp.clip(jnp.exp(jax.random.uniform(arg_keys[6], (D,), jnp.float32, math.log(0.5), math.log(2.0))), 0.5, 2.0)
    w_policy = normal_values(arg_keys[7], (D, ACT), D ** -0.5, 0.1875)
    return {"states": states, "member_of": member_of, "place": place, "norm_gain": norm_gain, "w_up": w_up, "w_down": w_down, "policy_gain": policy_gain, "w_policy": w_policy}


def rms_scale(values, gain):
    mean_square = lax.optimization_barrier(jnp.mean(values * values, axis=-1, keepdims=True))
    return values * lax.rsqrt(mean_square + 1e-06) * gain

def reference(states, member_of, place, norm_gain, w_up, w_down, policy_gain, w_policy):
    member = member_of[:, 0].astype(jnp.int32)
    order = jnp.argsort(member, stable=True).astype(jnp.int32)
    sorted_member = member[order]
    sorted_states = states[order]
    block_rows = min(256, ROWS)
    block_count = ROWS // block_rows

    def one_block(pair):
        block_states, block_member = pair
        base = block_states.astype(jnp.float32)

        def apply_member(member_id, running):
            up_whole = jnp.concatenate([w_up[2 * member_id], w_up[2 * member_id + 1]], axis=1)
            down_whole = jnp.concatenate([w_down[2 * member_id], w_down[2 * member_id + 1]], axis=0)
            normed = rms_scale(base, norm_gain[member_id]).astype(jnp.bfloat16)
            hidden = jax.nn.gelu(jnp.dot(normed, up_whole, preferred_element_type=jnp.float32)).astype(jnp.bfloat16)
            change = jnp.dot(hidden, down_whole, preferred_element_type=jnp.float32)
            return jnp.where((block_member == member_id)[:, None], change, running)
        change = lax.fori_loop(block_member[0], block_member[-1] + 1, apply_member, jnp.zeros(base.shape, jnp.float32))
        return (base + change).astype(jnp.bfloat16)
    predicted = lax.map(one_block, (sorted_states.reshape(block_count, block_rows, D), sorted_member.reshape(block_count, block_rows)))
    predicted = predicted.reshape(ROWS, D)
    imagined = jnp.zeros((ROWS, D), jnp.bfloat16).at[place[order]].set(predicted)
    policy_normed = rms_scale(imagined.astype(jnp.float32), policy_gain).astype(jnp.bfloat16)
    action = jnp.tanh(jnp.dot(policy_normed, w_policy, preferred_element_type=jnp.float32)).astype(jnp.bfloat16)
    return (imagined, action)
```

```python
import jax
import jax.numpy as jnp
from jax import lax
from jax.sharding import PartitionSpec as P


def from_partner(value, axis, distance):
    return lax.ppermute(value, axis, [(i, i ^ 1 << distance) for i in range(lax.axis_size(axis))])


def rms_scale(values, gain):
    mean_square = jnp.mean(values * values, axis=-1, keepdims=True)
    return values * lax.rsqrt(mean_square + 1e-06) * gain


def running_rank(member_hits):
    return jnp.sum((jnp.cumsum(member_hits, axis=0) - member_hits) * member_hits, axis=1)


def local(states, member_of, place, norm_gain, w_up, w_down, policy_gain, w_policy):
    n_member = lax.axis_size("member")
    n_tp = lax.axis_size("tp")
    n_dev = n_member * n_tp
    group_width = 2 * n_tp
    member_total = n_member // 2
    rows_here = states.shape[0]
    feature_width = states.shape[1]
    slot_count = 2 * rows_here // n_dev
    member = member_of[:, 0]
    member_hits = (member[:, None] == jnp.arange(member_total, dtype=jnp.int32)[None, :]).astype(
        jnp.int32
    )
    earlier = running_rank(member_hits)
    target = (member * group_width + earlier % group_width) * slot_count + earlier // group_width
    picker = (jnp.arange(n_dev * slot_count, dtype=jnp.int32)[:, None] == target[None, :]).astype(
        jnp.bfloat16
    )
    outgoing = jnp.dot(picker, states, preferred_element_type=jnp.float32).astype(jnp.bfloat16)
    arrived = lax.all_to_all(
        outgoing.reshape(n_dev, slot_count, feature_width),
        ("member", "tp"),
        split_axis=0,
        concat_axis=0,
        tiled=True,
    )
    arrived = arrived.reshape(n_dev * slot_count, feature_width)
    own_member = lax.axis_index("member") // 2
    gain_here = lax.dynamic_index_in_dim(norm_gain, own_member, 0, keepdims=False)
    normed = rms_scale(arrived.astype(jnp.float32), gain_here).astype(jnp.bfloat16)
    up_local = jnp.concatenate([w_up[0], from_partner(w_up[0], "member", 0)], axis=1)
    down_local = jnp.concatenate([w_down[0], from_partner(w_down[0], "member", 0)], axis=0)
    hidden = jax.nn.gelu(
        jnp.dot(
            lax.all_gather(normed, "tp", axis=0, tiled=True),
            up_local,
            preferred_element_type=jnp.float32,
        )
    ).astype(jnp.bfloat16)
    change = lax.psum_scatter(
        jnp.dot(hidden, down_local, preferred_element_type=jnp.float32),
        "tp",
        scatter_dimension=0,
        tiled=True,
    )
    predicted = (arrived.astype(jnp.float32) + change).astype(jnp.bfloat16)
    returned = lax.all_to_all(
        predicted.reshape(n_dev, slot_count, feature_width),
        ("member", "tp"),
        split_axis=0,
        concat_axis=0,
        tiled=True,
    )
    returned = returned.reshape(n_dev * slot_count, feature_width)
    own_rows = jnp.einsum("sr,sd->rd", picker, returned, preferred_element_type=jnp.float32).astype(
        jnp.bfloat16
    )
    per_learner = rows_here // n_dev
    learner = place // rows_here
    spot_index = place % rows_here
    learner_hits = (learner[:, None] == jnp.arange(n_dev, dtype=jnp.int32)[None, :]).astype(
        jnp.int32
    )
    lane_index = learner * per_learner + running_rank(learner_hits)
    placer = jnp.arange(rows_here, dtype=jnp.int32)[:, None] == lane_index[None, :]
    packed = jnp.dot(
        placer.astype(jnp.bfloat16), own_rows, preferred_element_type=jnp.float32
    ).astype(jnp.bfloat16)
    packed_spot = jnp.sum(placer.astype(jnp.int32) * spot_index[None, :], axis=1)
    arrivals, arrival_spots = (
        lax.all_to_all(
            packed.reshape(n_dev, per_learner, feature_width),
            ("member", "tp"),
            split_axis=0,
            concat_axis=0,
            tiled=True,
        ),
        lax.all_to_all(
            packed_spot.reshape(n_dev, per_learner),
            ("member", "tp"),
            split_axis=0,
            concat_axis=0,
            tiled=True,
        ),
    )
    arrivals = arrivals.reshape(rows_here, feature_width)
    arrival_spots = arrival_spots.reshape(rows_here)
    settle = (jnp.arange(rows_here, dtype=jnp.int32)[:, None] == arrival_spots[None, :]).astype(
        jnp.bfloat16
    )
    imagined = jnp.dot(settle, arrivals, preferred_element_type=jnp.float32).astype(jnp.bfloat16)
    policy_normed = rms_scale(imagined.astype(jnp.float32), policy_gain).astype(jnp.bfloat16)
    action = jnp.tanh(jnp.dot(policy_normed, w_policy, preferred_element_type=jnp.float32)).astype(
        jnp.bfloat16
    )
    return (imagined, action)


def solution(mesh):
    in_specs = (
        P(("rep", "member", "tp"), None),
        P(("rep", "member", "tp"), None),
        P(("rep", "member", "tp")),
        P(),
        P("member", None, "tp"),
        P("member", "tp", None),
        P(),
        P(),
    )
    out_specs = (P(("rep", "member", "tp"), None), P(("rep", "member", "tp"), None))
    return jax.shard_map(local, mesh=mesh, in_specs=in_specs, out_specs=out_specs, check_vma=False)
```

```python
import jax
import jax.numpy as jnp
from jax import lax
from jax.sharding import PartitionSpec as P


def from_partner(value, axis, distance):
    return lax.ppermute(value, axis, [(i, i ^ 1 << distance) for i in range(lax.axis_size(axis))])


def rms_scale(values, gain):
    mean_square = jnp.mean(values * values, axis=-1, keepdims=True)
    return values * lax.rsqrt(mean_square + 1e-06) * gain


def running_rank(member_hits):
    return jnp.sum((jnp.cumsum(member_hits, axis=0) - member_hits) * member_hits, axis=1)


def local(states, member_of, place, norm_gain, w_up, w_down, policy_gain, w_policy):
    n_member = lax.axis_size("member")
    n_tp = lax.axis_size("tp")
    n_dev = n_member * n_tp
    group_width = 2 * n_tp
    member_total = n_member // 2
    rows_here = states.shape[0]
    feature_width = states.shape[1]
    slot_count = 2 * rows_here // n_dev
    member = member_of[:, 0]
    member_hits = (member[:, None] == jnp.arange(member_total, dtype=jnp.int32)[None, :]).astype(
        jnp.int32
    )
    earlier = running_rank(member_hits)
    target = (member * group_width + earlier % group_width) * slot_count + earlier // group_width
    picker = (jnp.arange(n_dev * slot_count, dtype=jnp.int32)[:, None] == target[None, :]).astype(
        jnp.bfloat16
    )
    outgoing = jnp.dot(picker, states, preferred_element_type=jnp.float32).astype(jnp.bfloat16)
    arrived = lax.all_to_all(
        outgoing.reshape(n_dev, slot_count, feature_width),
        ("member", "tp"),
        split_axis=0,
        concat_axis=0,
        tiled=True,
    )
    arrived = arrived.reshape(n_dev * slot_count, feature_width)
    own_member = lax.axis_index("member") // 2
    gain_here = lax.dynamic_index_in_dim(norm_gain, own_member, 0, keepdims=False)
    normed = rms_scale(arrived.astype(jnp.float32), gain_here).astype(jnp.bfloat16)
    up_local = jnp.concatenate([w_up[0], from_partner(w_up[0], "member", 0)], axis=1)
    down_local = jnp.concatenate([w_down[0], from_partner(w_down[0], "member", 0)], axis=0)
    hidden = jax.nn.gelu(
        jnp.dot(
            lax.all_gather(normed, "tp", axis=0, tiled=True),
            up_local,
            preferred_element_type=jnp.float32,
        )
    ).astype(jnp.bfloat16)
    change = lax.psum_scatter(
        jnp.dot(hidden, down_local, preferred_element_type=jnp.float32).astype(jnp.bfloat16),
        "tp",
        scatter_dimension=0,
        tiled=True,
    ).astype(jnp.float32)
    predicted = (arrived.astype(jnp.float32) + change).astype(jnp.bfloat16)
    returned = lax.all_to_all(
        predicted.reshape(n_dev, slot_count, feature_width),
        ("member", "tp"),
        split_axis=0,
        concat_axis=0,
        tiled=True,
    )
    returned = returned.reshape(n_dev * slot_count, feature_width)
    own_rows = jnp.einsum("sr,sd->rd", picker, returned, preferred_element_type=jnp.float32).astype(
        jnp.bfloat16
    )
    per_learner = rows_here // n_dev
    learner = place // rows_here
    spot_index = place % rows_here
    learner_hits = (learner[:, None] == jnp.arange(n_dev, dtype=jnp.int32)[None, :]).astype(
        jnp.int32
    )
    lane_index = learner * per_learner + running_rank(learner_hits)
    placer = jnp.arange(rows_here, dtype=jnp.int32)[:, None] == lane_index[None, :]
    packed = jnp.dot(
        placer.astype(jnp.bfloat16), own_rows, preferred_element_type=jnp.float32
    ).astype(jnp.bfloat16)
    packed_spot = jnp.sum(placer.astype(jnp.int32) * spot_index[None, :], axis=1)
    arrivals, arrival_spots = (
        lax.all_to_all(
            packed.reshape(n_dev, per_learner, feature_width),
            ("member", "tp"),
            split_axis=0,
            concat_axis=0,
            tiled=True,
        ),
        lax.all_to_all(
            packed_spot.reshape(n_dev, per_learner),
            ("member", "tp"),
            split_axis=0,
            concat_axis=0,
            tiled=True,
        ),
    )
    arrivals = arrivals.reshape(rows_here, feature_width)
    arrival_spots = arrival_spots.reshape(rows_here)
    settle = (jnp.arange(rows_here, dtype=jnp.int32)[:, None] == arrival_spots[None, :]).astype(
        jnp.bfloat16
    )
    imagined = jnp.dot(settle, arrivals, preferred_element_type=jnp.float32).astype(jnp.bfloat16)
    policy_normed = rms_scale(imagined.astype(jnp.float32), policy_gain).astype(jnp.bfloat16)
    action = jnp.tanh(jnp.dot(policy_normed, w_policy, preferred_element_type=jnp.float32)).astype(
        jnp.bfloat16
    )
    return (imagined, action)


def solution(mesh):
    in_specs = (
        P(("rep", "member", "tp"), None),
        P(("rep", "member", "tp"), None),
        P(("rep", "member", "tp")),
        P(),
        P("member", None, "tp"),
        P("member", "tp", None),
        P(),
        P(),
    )
    out_specs = (P(("rep", "member", "tp"), None), P(("rep", "member", "tp"), None))
    return jax.shard_map(local, mesh=mesh, in_specs=in_specs, out_specs=out_specs, check_vma=False)
```

```python
import jax
import jax.numpy as jnp
from jax import lax
from jax.sharding import PartitionSpec as P


PARTIAL_DTYPE = jnp.float32


def from_partner(value, axis, distance):
    return lax.ppermute(value, axis, [(i, i ^ 1 << distance) for i in range(lax.axis_size(axis))])


def rms_scale(values, gain):
    mean_square = jnp.mean(values * values, axis=-1, keepdims=True)
    return values * lax.rsqrt(mean_square + 1e-06) * gain


def running_rank(member_hits):
    return jnp.sum((jnp.cumsum(member_hits, axis=0) - member_hits) * member_hits, axis=1)


def local(states, member_of, place, norm_gain, w_up, w_down, policy_gain, w_policy):
    n_member = lax.axis_size("member")
    n_tp = lax.axis_size("tp")
    n_dev = n_member * n_tp
    member_total = n_member // 2
    rows_here = states.shape[0]
    feature_width = states.shape[1]
    pair_slots = rows_here // member_total
    all_place = lax.all_gather(place, ("member", "tp"), axis=0, tiled=True)
    up_local = jnp.concatenate([w_up[0], from_partner(w_up[0], "member", 0)], axis=1)
    down_local = jnp.concatenate([w_down[0], from_partner(w_down[0], "member", 0)], axis=0)
    member = member_of[:, 0]
    member_hits = (member[:, None] == jnp.arange(member_total, dtype=jnp.int32)[None, :]).astype(
        jnp.int32
    )
    earlier = running_rank(member_hits)
    target = (2 * member + earlier % 2) * pair_slots + earlier // 2
    picker = (jnp.arange(n_member * pair_slots, dtype=jnp.int32)[:, None] == target[None, :]).astype(
        jnp.bfloat16
    )
    outgoing = jnp.dot(picker, states, preferred_element_type=jnp.float32).astype(jnp.bfloat16)
    arrived = lax.all_to_all(
        outgoing.reshape(n_member, pair_slots, feature_width),
        "member",
        split_axis=0,
        concat_axis=0,
        tiled=True,
    )
    arrived = arrived.reshape(n_member * pair_slots, feature_width)
    own_member = lax.axis_index("member") // 2
    gain_here = lax.dynamic_index_in_dim(norm_gain, own_member, 0, keepdims=False)
    normed = rms_scale(arrived.astype(jnp.float32), gain_here).astype(jnp.bfloat16)
    hidden = jax.nn.gelu(
        jnp.dot(
            lax.all_gather(normed, "tp", axis=0, tiled=True),
            up_local,
            preferred_element_type=jnp.float32,
        )
    ).astype(jnp.bfloat16)
    change = lax.psum_scatter(
        jnp.dot(hidden, down_local, preferred_element_type=jnp.float32).astype(PARTIAL_DTYPE),
        "tp",
        scatter_dimension=0,
        tiled=True,
    ).astype(jnp.float32)
    predicted = (arrived.astype(jnp.float32) + change).astype(jnp.bfloat16)
    returned = lax.all_to_all(
        predicted.reshape(n_member, pair_slots, feature_width),
        "member",
        split_axis=0,
        concat_axis=0,
        tiled=True,
    )
    returned = returned.reshape(n_member * pair_slots, feature_width)
    own_rows = jnp.einsum("sr,sd->rd", picker, returned, preferred_element_type=jnp.float32).astype(
        jnp.bfloat16
    )
    per_learner = rows_here // n_dev
    learner = place // rows_here
    learner_hits = (learner[:, None] == jnp.arange(n_dev, dtype=jnp.int32)[None, :]).astype(
        jnp.int32
    )
    lane_index = learner * per_learner + running_rank(learner_hits)
    placer = jnp.arange(rows_here, dtype=jnp.int32)[:, None] == lane_index[None, :]
    packed = jnp.dot(
        placer.astype(jnp.bfloat16), own_rows, preferred_element_type=jnp.float32
    ).astype(jnp.bfloat16)
    arrivals = lax.all_to_all(
        packed.reshape(n_dev, per_learner, feature_width),
        ("member", "tp"),
        split_axis=0,
        concat_axis=0,
        tiled=True,
    )
    arrivals = arrivals.reshape(n_dev * per_learner, feature_width)
    me = lax.axis_index("member") * n_tp + lax.axis_index("tp")
    source_place = all_place.reshape(n_dev, rows_here)
    mine = (source_place // rows_here == me).astype(jnp.int32)
    slot_of = (
        jnp.arange(n_dev, dtype=jnp.int32)[:, None] * per_learner
        + jnp.cumsum(mine, axis=1)
        - mine
    ).reshape(-1)
    spot_of = (source_place % rows_here).reshape(-1)
    mine = mine.reshape(-1)
    spot_pick = (
        (jnp.arange(rows_here, dtype=jnp.int32)[:, None] == spot_of[None, :]) & (mine[None, :] > 0)
    ).astype(jnp.bfloat16)
    slot_pick = (slot_of[:, None] == jnp.arange(n_dev * per_learner, dtype=jnp.int32)[None, :]).astype(
        jnp.bfloat16
    )
    settle = jnp.dot(spot_pick, slot_pick, preferred_element_type=jnp.float32).astype(jnp.bfloat16)
    imagined = jnp.dot(settle, arrivals, preferred_element_type=jnp.float32).astype(jnp.bfloat16)
    policy_normed = rms_scale(imagined.astype(jnp.float32), policy_gain).astype(jnp.bfloat16)
    action = jnp.tanh(jnp.dot(policy_normed, w_policy, preferred_element_type=jnp.float32)).astype(
        jnp.bfloat16
    )
    return (imagined, action)


def solution(mesh):
    in_specs = (
        P(("rep", "member", "tp"), None),
        P(("rep", "member", "tp"), None),
        P(("rep", "member", "tp")),
        P(),
        P("member", None, "tp"),
        P("member", "tp", None),
        P(),
        P(),
    )
    out_specs = (P(("rep", "member", "tp"), None), P(("rep", "member", "tp"), None))
    return jax.shard_map(local, mesh=mesh, in_specs=in_specs, out_specs=out_specs, check_vma=False)
```

```python
import jax
import jax.numpy as jnp
from jax import lax
from jax.sharding import PartitionSpec as P


PARTIAL_DTYPE = jnp.float32


def from_partner(value, axis, distance):
    return lax.ppermute(value, axis, [(i, i ^ 1 << distance) for i in range(lax.axis_size(axis))])


def rms_scale(values, gain):
    mean_square = jnp.mean(values * values, axis=-1, keepdims=True)
    return values * lax.rsqrt(mean_square + 1e-06) * gain


def running_rank(member_hits):
    return jnp.sum((jnp.cumsum(member_hits, axis=0) - member_hits) * member_hits, axis=1)


def local(states, member_of, place, norm_gain, w_up, w_down, policy_gain, w_policy):
    n_member = lax.axis_size("member")
    n_tp = lax.axis_size("tp")
    n_dev = n_member * n_tp
    member_total = n_member // 2
    rows_here = states.shape[0]
    feature_width = states.shape[1]
    pair_slots = rows_here // member_total
    up_local = jnp.concatenate([w_up[0], from_partner(w_up[0], "member", 0)], axis=1)
    down_local = jnp.concatenate([w_down[0], from_partner(w_down[0], "member", 0)], axis=0)
    member = member_of[:, 0]
    member_hits = (member[:, None] == jnp.arange(member_total, dtype=jnp.int32)[None, :]).astype(
        jnp.int32
    )
    earlier = running_rank(member_hits)
    target = (2 * member + earlier % 2) * pair_slots + earlier // 2
    picker = (jnp.arange(n_member * pair_slots, dtype=jnp.int32)[:, None] == target[None, :]).astype(
        jnp.bfloat16
    )
    outgoing = jnp.dot(picker, states, preferred_element_type=jnp.float32).astype(jnp.bfloat16)
    arrived = lax.all_to_all(
        outgoing.reshape(n_member, pair_slots, feature_width),
        "member",
        split_axis=0,
        concat_axis=0,
        tiled=True,
    )
    arrived = arrived.reshape(n_member * pair_slots, feature_width)
    own_member = lax.axis_index("member") // 2
    gain_here = lax.dynamic_index_in_dim(norm_gain, own_member, 0, keepdims=False)
    normed = rms_scale(arrived.astype(jnp.float32), gain_here).astype(jnp.bfloat16)
    hidden = jax.nn.gelu(
        jnp.dot(
            lax.all_gather(normed, "tp", axis=0, tiled=True),
            up_local,
            preferred_element_type=jnp.float32,
        )
    ).astype(jnp.bfloat16)
    change = lax.psum_scatter(
        jnp.dot(hidden, down_local, preferred_element_type=jnp.float32).astype(PARTIAL_DTYPE),
        "tp",
        scatter_dimension=0,
        tiled=True,
    ).astype(jnp.float32)
    predicted = (arrived.astype(jnp.float32) + change).astype(jnp.bfloat16)
    returned = lax.all_to_all(
        predicted.reshape(n_member, pair_slots, feature_width),
        "member",
        split_axis=0,
        concat_axis=0,
        tiled=True,
    )
    returned = returned.reshape(n_member * pair_slots, feature_width)
    own_rows = jnp.einsum("sr,sd->rd", picker, returned, preferred_element_type=jnp.float32).astype(
        jnp.bfloat16
    )
    per_learner = rows_here // n_dev
    learner = place // rows_here
    learner_hits = (learner[:, None] == jnp.arange(n_dev, dtype=jnp.int32)[None, :]).astype(
        jnp.int32
    )
    lane_index = learner * per_learner + running_rank(learner_hits)
    placer = jnp.arange(rows_here, dtype=jnp.int32)[:, None] == lane_index[None, :]
    spot_index = place % rows_here
    packed = jnp.dot(
        placer.astype(jnp.bfloat16), own_rows, preferred_element_type=jnp.float32
    ).astype(jnp.bfloat16)
    packed_spot = jnp.sum(placer.astype(jnp.int32) * spot_index[None, :], axis=1)
    spot_lanes = jnp.where(
        jnp.arange(128, dtype=jnp.int32)[None, :] == 0, packed_spot[:, None], 0
    ).astype(jnp.bfloat16)
    arrivals = lax.all_to_all(
        jnp.concatenate([packed, spot_lanes], axis=1).reshape(n_dev, per_learner, feature_width + 128),
        ("member", "tp"),
        split_axis=0,
        concat_axis=0,
        tiled=True,
    )
    arrivals = arrivals.reshape(n_dev * per_learner, feature_width + 128)
    arrival_spots = arrivals[:, feature_width].astype(jnp.int32)
    settle = (jnp.arange(rows_here, dtype=jnp.int32)[:, None] == arrival_spots[None, :]).astype(
        jnp.bfloat16
    )
    imagined = jnp.dot(
        settle, arrivals[:, :feature_width], preferred_element_type=jnp.float32
    ).astype(jnp.bfloat16)
    policy_normed = rms_scale(imagined.astype(jnp.float32), policy_gain).astype(jnp.bfloat16)
    action = jnp.tanh(jnp.dot(policy_normed, w_policy, preferred_element_type=jnp.float32)).astype(
        jnp.bfloat16
    )
    return (imagined, action)


def solution(mesh):
    in_specs = (
        P(("rep", "member", "tp"), None),
        P(("rep", "member", "tp"), None),
        P(("rep", "member", "tp")),
        P(),
        P("member", None, "tp"),
        P("member", "tp", None),
        P(),
        P(),
    )
    out_specs = (P(("rep", "member", "tp"), None), P(("rep", "member", "tp"), None))
    return jax.shard_map(local, mesh=mesh, in_specs=in_specs, out_specs=out_specs, check_vma=False)
```

```python
import jax
import jax.numpy as jnp
from jax import lax
from jax.sharding import PartitionSpec as P

PARTIAL_DTYPE = jnp.float32


def from_partner(value, axis, distance):
    return lax.ppermute(value, axis, [(i, i ^ 1 << distance) for i in range(lax.axis_size(axis))])


def from_chip_behind(value, axis, chips_back):
    size = lax.axis_size(axis)
    return lax.ppermute(value, axis, [(i, (i + 2 * chips_back) % size) for i in range(size)])


def rms_scale(values, gain):
    mean_square = jnp.mean(values * values, axis=-1, keepdims=True)
    return values * lax.rsqrt(mean_square + 1e-06) * gain


def running_rank(member_hits):
    return jnp.sum((jnp.cumsum(member_hits, axis=0) - member_hits) * member_hits, axis=1)


def local(states, member_of, place, norm_gain, w_up, w_down, policy_gain, w_policy):
    n_member = lax.axis_size("member")
    n_tp = lax.axis_size("tp")
    n_dev = n_member * n_tp
    member_total = n_member // 2
    rows_here = states.shape[0]
    feature_width = states.shape[1]
    own_member = lax.axis_index("member") // 2
    blocks = []
    for back in range(member_total):
        if back == 0:
            up_here, down_here = w_up[0], w_down[0]
        else:
            up_here = from_chip_behind(w_up[0], "member", back)
            down_here = from_chip_behind(w_down[0], "member", back)
        block_member = (own_member - back + member_total) % member_total
        blocks.append((block_member, up_here, down_here))
        blocks.append(
            (block_member, from_partner(up_here, "member", 0), from_partner(down_here, "member", 0))
        )
    member = member_of[:, 0]
    gain_rows = jnp.take(norm_gain, member, axis=0)
    normed = rms_scale(states.astype(jnp.float32), gain_rows).astype(jnp.bfloat16)
    member_lanes = jnp.where(
        jnp.arange(128, dtype=jnp.int32)[None, :] == 0, member[:, None], 0
    ).astype(jnp.bfloat16)
    gathered = lax.all_gather(
        jnp.concatenate([normed, member_lanes], axis=1), "tp", axis=0, tiled=True
    )
    gathered_rows = gathered[:, :feature_width]
    gathered_member = gathered[:, feature_width].astype(jnp.int32)
    partial = None
    for block_member, up_here, down_here in blocks:
        keep = (gathered_member == block_member).astype(jnp.bfloat16)[:, None]
        hidden = jax.nn.gelu(
            jnp.dot(gathered_rows, up_here, preferred_element_type=jnp.float32)
        ).astype(jnp.bfloat16) * keep
        term = jnp.dot(hidden, down_here, preferred_element_type=jnp.float32)
        partial = term if partial is None else partial + term
    change = lax.psum_scatter(
        partial.astype(PARTIAL_DTYPE), "tp", scatter_dimension=0, tiled=True
    ).astype(jnp.float32)
    own_rows = (states.astype(jnp.float32) + change).astype(jnp.bfloat16)
    per_learner = rows_here // n_dev
    learner = place // rows_here
    learner_hits = (learner[:, None] == jnp.arange(n_dev, dtype=jnp.int32)[None, :]).astype(
        jnp.int32
    )
    lane_index = learner * per_learner + running_rank(learner_hits)
    placer = jnp.arange(rows_here, dtype=jnp.int32)[:, None] == lane_index[None, :]
    spot_index = place % rows_here
    packed = jnp.dot(
        placer.astype(jnp.bfloat16), own_rows, preferred_element_type=jnp.float32
    ).astype(jnp.bfloat16)
    packed_spot = jnp.sum(placer.astype(jnp.int32) * spot_index[None, :], axis=1)
    spot_lanes = jnp.where(
        jnp.arange(128, dtype=jnp.int32)[None, :] == 0, packed_spot[:, None], 0
    ).astype(jnp.bfloat16)
    arrivals = lax.all_to_all(
        jnp.concatenate([packed, spot_lanes], axis=1).reshape(n_dev, per_learner, feature_width + 128),
        ("member", "tp"),
        split_axis=0,
        concat_axis=0,
        tiled=True,
    )
    arrivals = arrivals.reshape(n_dev * per_learner, feature_width + 128)
    arrival_spots = arrivals[:, feature_width].astype(jnp.int32)
    settle = (jnp.arange(rows_here, dtype=jnp.int32)[:, None] == arrival_spots[None, :]).astype(
        jnp.bfloat16
    )
    imagined = jnp.dot(
        settle, arrivals[:, :feature_width], preferred_element_type=jnp.float32
    ).astype(jnp.bfloat16)
    policy_normed = rms_scale(imagined.astype(jnp.float32), policy_gain).astype(jnp.bfloat16)
    action = jnp.tanh(jnp.dot(policy_normed, w_policy, preferred_element_type=jnp.float32)).astype(
        jnp.bfloat16
    )
    return (imagined, action)


def solution(mesh):
    in_specs = (
        P(("rep", "member", "tp"), None),
        P(("rep", "member", "tp"), None),
        P(("rep", "member", "tp")),
        P(),
        P("member", None, "tp"),
        P("member", "tp", None),
        P(),
        P(),
    )
    out_specs = (P(("rep", "member", "tp"), None), P(("rep", "member", "tp"), None))
    return jax.shard_map(local, mesh=mesh, in_specs=in_specs, out_specs=out_specs, check_vma=False)
```

```python
import jax
import jax.numpy as jnp
from jax import lax
from jax.sharding import PartitionSpec as P

PARTIAL_DTYPE = jnp.float32


def from_partner(value, axis, distance):
    return lax.ppermute(value, axis, [(i, i ^ 1 << distance) for i in range(lax.axis_size(axis))])


def from_chip_behind(value, axis, chips_back):
    size = lax.axis_size(axis)
    return lax.ppermute(value, axis, [(i, (i + 2 * chips_back) % size) for i in range(size)])


def rms_scale(values, gain):
    mean_square = jnp.mean(values * values, axis=-1, keepdims=True)
    return values * lax.rsqrt(mean_square + 1e-06) * gain


def running_rank(member_hits):
    return jnp.sum((jnp.cumsum(member_hits, axis=0) - member_hits) * member_hits, axis=1)


def local(states, member_of, place, norm_gain, w_up, w_down, policy_gain, w_policy):
    n_member = lax.axis_size("member")
    n_tp = lax.axis_size("tp")
    n_dev = n_member * n_tp
    member_total = n_member // 2
    rows_here = states.shape[0]
    feature_width = states.shape[1]
    own_member = lax.axis_index("member") // 2
    own_block = (own_member, w_up[0], w_down[0])
    fetched = [
        (
            (own_member - back + member_total) % member_total,
            from_chip_behind(w_up[0], "member", back),
            from_chip_behind(w_down[0], "member", back),
        )
        for back in range(1, member_total)
    ]
    member = member_of[:, 0]
    gain_rows = jnp.take(norm_gain, member, axis=0)
    normed = rms_scale(states.astype(jnp.float32), gain_rows).astype(jnp.bfloat16)
    member_lanes = jnp.where(
        jnp.arange(128, dtype=jnp.int32)[None, :] == 0, member[:, None], 0
    ).astype(jnp.bfloat16)
    gathered = lax.all_gather(
        jnp.concatenate([normed, member_lanes], axis=1), "tp", axis=0, tiled=True
    )
    gathered_rows = gathered[:, :feature_width]
    gathered_member = gathered[:, feature_width].astype(jnp.int32)

    def apply_block(block_member, up_here, down_here):
        keep = (gathered_member == block_member).astype(jnp.bfloat16)[:, None]
        hidden = jax.nn.gelu(
            jnp.dot(gathered_rows, up_here, preferred_element_type=jnp.float32)
        ).astype(jnp.bfloat16) * keep
        return jnp.dot(hidden, down_here, preferred_element_type=jnp.float32)

    def apply_pair(block_member, up_here, down_here):
        return apply_block(block_member, up_here, down_here) + apply_block(
            block_member, from_partner(up_here, "member", 0), from_partner(down_here, "member", 0)
        )

    partial = apply_pair(*own_block)
    for block_member, up_here, down_here in fetched:
        partial, up_here, down_here = lax.optimization_barrier((partial, up_here, down_here))
        partial = partial + apply_pair(block_member, up_here, down_here)
    change = lax.psum_scatter(
        partial.astype(PARTIAL_DTYPE), "tp", scatter_dimension=0, tiled=True
    ).astype(jnp.float32)
    own_rows = (states.astype(jnp.float32) + change).astype(jnp.bfloat16)
    per_learner = rows_here // n_dev
    learner = place // rows_here
    learner_hits = (learner[:, None] == jnp.arange(n_dev, dtype=jnp.int32)[None, :]).astype(
        jnp.int32
    )
    lane_index = learner * per_learner + running_rank(learner_hits)
    placer = jnp.arange(rows_here, dtype=jnp.int32)[:, None] == lane_index[None, :]
    spot_index = place % rows_here
    packed = jnp.dot(
        placer.astype(jnp.bfloat16), own_rows, preferred_element_type=jnp.float32
    ).astype(jnp.bfloat16)
    packed_spot = jnp.sum(placer.astype(jnp.int32) * spot_index[None, :], axis=1)
    spot_lanes = jnp.where(
        jnp.arange(128, dtype=jnp.int32)[None, :] == 0, packed_spot[:, None], 0
    ).astype(jnp.bfloat16)
    arrivals = lax.all_to_all(
        jnp.concatenate([packed, spot_lanes], axis=1).reshape(n_dev, per_learner, feature_width + 128),
        ("member", "tp"),
        split_axis=0,
        concat_axis=0,
        tiled=True,
    )
    arrivals = arrivals.reshape(n_dev * per_learner, feature_width + 128)
    arrival_spots = arrivals[:, feature_width].astype(jnp.int32)
    settle = (jnp.arange(rows_here, dtype=jnp.int32)[:, None] == arrival_spots[None, :]).astype(
        jnp.bfloat16
    )
    imagined = jnp.dot(
        settle, arrivals[:, :feature_width], preferred_element_type=jnp.float32
    ).astype(jnp.bfloat16)
    policy_normed = rms_scale(imagined.astype(jnp.float32), policy_gain).astype(jnp.bfloat16)
    action = jnp.tanh(jnp.dot(policy_normed, w_policy, preferred_element_type=jnp.float32)).astype(
        jnp.bfloat16
    )
    return (imagined, action)


def solution(mesh):
    in_specs = (
        P(("rep", "member", "tp"), None),
        P(("rep", "member", "tp"), None),
        P(("rep", "member", "tp")),
        P(),
        P("member", None, "tp"),
        P("member", "tp", None),
        P(),
        P(),
    )
    out_specs = (P(("rep", "member", "tp"), None), P(("rep", "member", "tp"), None))
    return jax.shard_map(local, mesh=mesh, in_specs=in_specs, out_specs=out_specs, check_vma=False)
```

```python
import jax
import jax.numpy as jnp
from jax import lax
from jax.sharding import PartitionSpec as P

PARTIAL_DTYPE = jnp.float32


def from_partner(value, axis, distance):
    return lax.ppermute(value, axis, [(i, i ^ 1 << distance) for i in range(lax.axis_size(axis))])


def from_chip_behind(value, axis, chips_back):
    size = lax.axis_size(axis)
    return lax.ppermute(value, axis, [(i, (i + 2 * chips_back) % size) for i in range(size)])


def rms_scale(values, gain):
    mean_square = jnp.mean(values * values, axis=-1, keepdims=True)
    return values * lax.rsqrt(mean_square + 1e-06) * gain


def running_rank(member_hits):
    return jnp.sum((jnp.cumsum(member_hits, axis=0) - member_hits) * member_hits, axis=1)


def lane_column(values):
    return jnp.where(jnp.arange(128, dtype=jnp.int32)[None, :] == 0, values[:, None], 0).astype(
        jnp.bfloat16
    )


def local(states, member_of, place, norm_gain, w_up, w_down, policy_gain, w_policy):
    n_member = lax.axis_size("member")
    n_tp = lax.axis_size("tp")
    n_dev = n_member * n_tp
    member_total = n_member // 2
    rows_here = states.shape[0]
    feature_width = states.shape[1]
    per_learner = rows_here // n_dev
    chunks = 2 if per_learner % 2 == 0 else 1
    per_chunk = per_learner // chunks
    chunk_rows = rows_here // chunks
    own_member = lax.axis_index("member") // 2
    own_block = (own_member, w_up[0], w_down[0])
    fetched = [
        (
            (own_member - back + member_total) % member_total,
            from_chip_behind(w_up[0], "member", back),
            from_chip_behind(w_down[0], "member", back),
        )
        for back in range(1, member_total)
    ]
    learner = place // rows_here
    learner_hits = (learner[:, None] == jnp.arange(n_dev, dtype=jnp.int32)[None, :]).astype(
        jnp.int32
    )
    rank = running_rank(learner_hits)
    slot = (rank // per_chunk) * chunk_rows + learner * per_chunk + rank % per_chunk
    slot_hits = jnp.arange(rows_here, dtype=jnp.int32)[:, None] == slot[None, :]
    sorted_states = jnp.dot(
        slot_hits.astype(jnp.bfloat16), states, preferred_element_type=jnp.float32
    ).astype(jnp.bfloat16)
    sorted_member = jnp.sum(slot_hits.astype(jnp.int32) * member_of[:, 0][None, :], axis=1)
    sorted_spot = jnp.sum(slot_hits.astype(jnp.int32) * (place % rows_here)[None, :], axis=1)
    gain_rows = jnp.take(norm_gain, sorted_member, axis=0)
    normed = rms_scale(sorted_states.astype(jnp.float32), gain_rows).astype(jnp.bfloat16)
    gathered = lax.all_gather(
        jnp.concatenate([normed, lane_column(sorted_member)], axis=1), "tp", axis=0, tiled=True
    ).reshape(n_tp, chunks, chunk_rows, feature_width + 128)

    def apply_block(chunk, block_member, up_here, down_here):
        rows = chunk[:, :feature_width]
        keep = (chunk[:, feature_width].astype(jnp.int32) == block_member).astype(jnp.bfloat16)
        hidden = jax.nn.gelu(
            jnp.dot(rows, up_here, preferred_element_type=jnp.float32)
        ).astype(jnp.bfloat16) * keep[:, None]
        return jnp.dot(hidden, down_here, preferred_element_type=jnp.float32)

    def apply_pair(chunk, block_member, up_here, down_here):
        return apply_block(chunk, block_member, up_here, down_here) + apply_block(
            chunk, block_member, from_partner(up_here, "member", 0), from_partner(down_here, "member", 0)
        )

    chunk_inputs = [
        gathered[:, c].reshape(n_tp * chunk_rows, feature_width + 128) for c in range(chunks)
    ]
    partials = [apply_pair(chunk, *own_block) for chunk in chunk_inputs]
    for block_member, up_here, down_here in fetched:
        partials, up_here, down_here = lax.optimization_barrier((partials, up_here, down_here))
        partials = [
            partial + apply_pair(chunk, block_member, up_here, down_here)
            for partial, chunk in zip(partials, chunk_inputs)
        ]
    changes = [
        lax.psum_scatter(partial.astype(PARTIAL_DTYPE), "tp", scatter_dimension=0, tiled=True)
        for partial in partials
    ]
    arrivals = []
    for c in range(chunks):
        change = changes[c].astype(jnp.float32)
        rows_out = sorted_states[c * chunk_rows:(c + 1) * chunk_rows]
        predicted = (rows_out.astype(jnp.float32) + change).astype(jnp.bfloat16)
        spots_out = lane_column(sorted_spot[c * chunk_rows:(c + 1) * chunk_rows])
        arrivals.append(
            lax.all_to_all(
                jnp.concatenate([predicted, spots_out], axis=1).reshape(
                    n_dev, per_chunk, feature_width + 128
                ),
                ("member", "tp"),
                split_axis=0,
                concat_axis=0,
                tiled=True,
            ).reshape(n_dev * per_chunk, feature_width + 128)
        )
        if c + 1 < chunks:
            arrivals[c], changes[c + 1] = lax.optimization_barrier((arrivals[c], changes[c + 1]))
    arrivals = jnp.concatenate(arrivals, axis=0)
    arrival_spots = arrivals[:, feature_width].astype(jnp.int32)
    settle = (jnp.arange(rows_here, dtype=jnp.int32)[:, None] == arrival_spots[None, :]).astype(
        jnp.bfloat16
    )
    imagined = jnp.dot(
        settle, arrivals[:, :feature_width], preferred_element_type=jnp.float32
    ).astype(jnp.bfloat16)
    policy_normed = rms_scale(imagined.astype(jnp.float32), policy_gain).astype(jnp.bfloat16)
    action = jnp.tanh(jnp.dot(policy_normed, w_policy, preferred_element_type=jnp.float32)).astype(
        jnp.bfloat16
    )
    return (imagined, action)


def solution(mesh):
    in_specs = (
        P(("rep", "member", "tp"), None),
        P(("rep", "member", "tp"), None),
        P(("rep", "member", "tp")),
        P(),
        P("member", None, "tp"),
        P("member", "tp", None),
        P(),
        P(),
    )
    out_specs = (P(("rep", "member", "tp"), None), P(("rep", "member", "tp"), None))
    return jax.shard_map(local, mesh=mesh, in_specs=in_specs, out_specs=out_specs, check_vma=False)
```

```python
import jax
import jax.numpy as jnp
from jax import lax
from jax.sharding import PartitionSpec as P

PARTIAL_DTYPE = jnp.float32


def from_partner(value, axis, distance):
    return lax.ppermute(value, axis, [(i, i ^ 1 << distance) for i in range(lax.axis_size(axis))])


def from_chip_behind(value, axis, chips_back):
    size = lax.axis_size(axis)
    return lax.ppermute(value, axis, [(i, (i + 2 * chips_back) % size) for i in range(size)])


def rms_scale(values, gain):
    mean_square = jnp.mean(values * values, axis=-1, keepdims=True)
    return values * lax.rsqrt(mean_square + 1e-06) * gain


def running_rank(member_hits):
    return jnp.sum((jnp.cumsum(member_hits, axis=0) - member_hits) * member_hits, axis=1)


def local(states, member_of, place, norm_gain, w_up, w_down, policy_gain, w_policy):
    n_member = lax.axis_size("member")
    n_tp = lax.axis_size("tp")
    n_dev = n_member * n_tp
    member_total = n_member // 2
    rows_here = states.shape[0]
    feature_width = states.shape[1]
    own_member = lax.axis_index("member") // 2
    own_block = (own_member, w_up[0], w_down[0])
    fetched = []
    for back in range(1, member_total):
        up_here = from_chip_behind(w_up[0], "member", back)
        up_here, down_source = lax.optimization_barrier((up_here, w_down[0]))
        down_here = from_chip_behind(down_source, "member", back)
        fetched.append(((own_member - back + member_total) % member_total, up_here, down_here))
    member = member_of[:, 0]
    gain_rows = jnp.take(norm_gain, member, axis=0)
    normed = rms_scale(states.astype(jnp.float32), gain_rows).astype(jnp.bfloat16)
    member_lanes = jnp.where(
        jnp.arange(128, dtype=jnp.int32)[None, :] == 0, member[:, None], 0
    ).astype(jnp.bfloat16)
    gathered = lax.all_gather(
        jnp.concatenate([normed, member_lanes], axis=1), "tp", axis=0, tiled=True
    )
    gathered_rows = gathered[:, :feature_width]
    gathered_member = gathered[:, feature_width].astype(jnp.int32)

    def hidden_of(block_member, up_here):
        keep = (gathered_member == block_member).astype(jnp.bfloat16)[:, None]
        return jax.nn.gelu(
            jnp.dot(gathered_rows, up_here, preferred_element_type=jnp.float32)
        ).astype(jnp.bfloat16) * keep

    def apply_pair(block_member, up_here, down_here):
        first = hidden_of(block_member, up_here)
        second = hidden_of(block_member, from_partner(up_here, "member", 0))
        return jnp.dot(first, down_here, preferred_element_type=jnp.float32) + jnp.dot(
            second, from_partner(down_here, "member", 0), preferred_element_type=jnp.float32
        )

    partial = apply_pair(*own_block)
    for block_member, up_here, down_here in fetched:
        partial, up_here = lax.optimization_barrier((partial, up_here))
        first = hidden_of(block_member, up_here)
        second = hidden_of(block_member, from_partner(up_here, "member", 0))
        first, second, down_here = lax.optimization_barrier((first, second, down_here))
        partial = (
            partial
            + jnp.dot(first, down_here, preferred_element_type=jnp.float32)
            + jnp.dot(second, from_partner(down_here, "member", 0), preferred_element_type=jnp.float32)
        )
    change = lax.psum_scatter(
        partial.astype(PARTIAL_DTYPE), "tp", scatter_dimension=0, tiled=True
    ).astype(jnp.float32)
    own_rows = (states.astype(jnp.float32) + change).astype(jnp.bfloat16)
    per_learner = rows_here // n_dev
    learner = place // rows_here
    learner_hits = (learner[:, None] == jnp.arange(n_dev, dtype=jnp.int32)[None, :]).astype(
        jnp.int32
    )
    lane_index = learner * per_learner + running_rank(learner_hits)
    placer = jnp.arange(rows_here, dtype=jnp.int32)[:, None] == lane_index[None, :]
    spot_index = place % rows_here
    packed = jnp.dot(
        placer.astype(jnp.bfloat16), own_rows, preferred_element_type=jnp.float32
    ).astype(jnp.bfloat16)
    packed_spot = jnp.sum(placer.astype(jnp.int32) * spot_index[None, :], axis=1)
    spot_lanes = jnp.where(
        jnp.arange(128, dtype=jnp.int32)[None, :] == 0, packed_spot[:, None], 0
    ).astype(jnp.bfloat16)
    arrivals = lax.all_to_all(
        jnp.concatenate([packed, spot_lanes], axis=1).reshape(n_dev, per_learner, feature_width + 128),
        ("member", "tp"),
        split_axis=0,
        concat_axis=0,
        tiled=True,
    )
    arrivals = arrivals.reshape(n_dev * per_learner, feature_width + 128)
    arrival_spots = arrivals[:, feature_width].astype(jnp.int32)
    settle = (jnp.arange(rows_here, dtype=jnp.int32)[:, None] == arrival_spots[None, :]).astype(
        jnp.bfloat16
    )
    imagined = jnp.dot(
        settle, arrivals[:, :feature_width], preferred_element_type=jnp.float32
    ).astype(jnp.bfloat16)
    policy_normed = rms_scale(imagined.astype(jnp.float32), policy_gain).astype(jnp.bfloat16)
    action = jnp.tanh(jnp.dot(policy_normed, w_policy, preferred_element_type=jnp.float32)).astype(
        jnp.bfloat16
    )
    return (imagined, action)


def solution(mesh):
    in_specs = (
        P(("rep", "member", "tp"), None),
        P(("rep", "member", "tp"), None),
        P(("rep", "member", "tp")),
        P(),
        P("member", None, "tp"),
        P("member", "tp", None),
        P(),
        P(),
    )
    out_specs = (P(("rep", "member", "tp"), None), P(("rep", "member", "tp"), None))
    return jax.shard_map(local, mesh=mesh, in_specs=in_specs, out_specs=out_specs, check_vma=False)
```

```python
import jax
import jax.numpy as jnp
from jax import lax
from jax.sharding import PartitionSpec as P

PARTIAL_DTYPE = jnp.bfloat16


def from_partner(value, axis, distance):
    return lax.ppermute(value, axis, [(i, i ^ 1 << distance) for i in range(lax.axis_size(axis))])


def from_chip_behind(value, axis, chips_back):
    size = lax.axis_size(axis)
    return lax.ppermute(value, axis, [(i, (i + 2 * chips_back) % size) for i in range(size)])


def rms_scale(values, gain):
    mean_square = jnp.mean(values * values, axis=-1, keepdims=True)
    return values * lax.rsqrt(mean_square + 1e-06) * gain


def running_rank(member_hits):
    return jnp.sum((jnp.cumsum(member_hits, axis=0) - member_hits) * member_hits, axis=1)


def local(states, member_of, place, norm_gain, w_up, w_down, policy_gain, w_policy):
    n_member = lax.axis_size("member")
    n_tp = lax.axis_size("tp")
    n_dev = n_member * n_tp
    member_total = n_member // 2
    rows_here = states.shape[0]
    feature_width = states.shape[1]
    own_member = lax.axis_index("member") // 2
    own_block = (own_member, w_up[0], w_down[0])
    fetched = [
        (
            (own_member - back + member_total) % member_total,
            from_chip_behind(w_up[0], "member", back),
            from_chip_behind(w_down[0], "member", back),
        )
        for back in range(1, member_total)
    ]
    member = member_of[:, 0]
    gain_rows = jnp.take(norm_gain, member, axis=0)
    normed = rms_scale(states.astype(jnp.float32), gain_rows).astype(jnp.bfloat16)
    member_lanes = jnp.where(
        jnp.arange(128, dtype=jnp.int32)[None, :] == 0, member[:, None], 0
    ).astype(jnp.bfloat16)
    gathered = lax.all_gather(
        jnp.concatenate([normed, member_lanes], axis=1), "tp", axis=0, tiled=True
    )
    gathered_rows = gathered[:, :feature_width]
    gathered_member = gathered[:, feature_width].astype(jnp.int32)

    def apply_block(block_member, up_here, down_here):
        keep = (gathered_member == block_member).astype(jnp.bfloat16)[:, None]
        hidden = jax.nn.gelu(
            jnp.dot(gathered_rows, up_here, preferred_element_type=jnp.float32)
        ).astype(jnp.bfloat16) * keep
        return jnp.dot(hidden, down_here, preferred_element_type=jnp.float32)

    def apply_pair(block_member, up_here, down_here):
        return apply_block(block_member, up_here, down_here) + apply_block(
            block_member, from_partner(up_here, "member", 0), from_partner(down_here, "member", 0)
        )

    partial = apply_pair(*own_block)
    for block_member, up_here, down_here in fetched:
        partial, up_here, down_here = lax.optimization_barrier((partial, up_here, down_here))
        partial = partial + apply_pair(block_member, up_here, down_here)
    tp_here = lax.axis_index("tp")
    by_target = partial.reshape(n_tp, rows_here, feature_width)
    change = lax.dynamic_index_in_dim(by_target, tp_here, 0, keepdims=False)
    for shift in range(1, n_tp):
        outgoing = lax.dynamic_index_in_dim(by_target, (tp_here + shift) % n_tp, 0, keepdims=False)
        change = change + lax.ppermute(
            outgoing.astype(PARTIAL_DTYPE),
            "tp",
            [(i, (i + shift) % n_tp) for i in range(n_tp)],
        ).astype(jnp.float32)
    own_rows = (states.astype(jnp.float32) + change).astype(jnp.bfloat16)
    per_learner = rows_here // n_dev
    learner = place // rows_here
    learner_hits = (learner[:, None] == jnp.arange(n_dev, dtype=jnp.int32)[None, :]).astype(
        jnp.int32
    )
    lane_index = learner * per_learner + running_rank(learner_hits)
    placer = jnp.arange(rows_here, dtype=jnp.int32)[:, None] == lane_index[None, :]
    spot_index = place % rows_here
    packed = jnp.dot(
        placer.astype(jnp.bfloat16), own_rows, preferred_element_type=jnp.float32
    ).astype(jnp.bfloat16)
    packed_spot = jnp.sum(placer.astype(jnp.int32) * spot_index[None, :], axis=1)
    spot_lanes = jnp.where(
        jnp.arange(128, dtype=jnp.int32)[None, :] == 0, packed_spot[:, None], 0
    ).astype(jnp.bfloat16)
    arrivals = lax.all_to_all(
        jnp.concatenate([packed, spot_lanes], axis=1).reshape(n_dev, per_learner, feature_width + 128),
        ("member", "tp"),
        split_axis=0,
        concat_axis=0,
        tiled=True,
    )
    arrivals = arrivals.reshape(n_dev * per_learner, feature_width + 128)
    arrival_spots = arrivals[:, feature_width].astype(jnp.int32)
    settle = (jnp.arange(rows_here, dtype=jnp.int32)[:, None] == arrival_spots[None, :]).astype(
        jnp.bfloat16
    )
    imagined = jnp.dot(
        settle, arrivals[:, :feature_width], preferred_element_type=jnp.float32
    ).astype(jnp.bfloat16)
    policy_normed = rms_scale(imagined.astype(jnp.float32), policy_gain).astype(jnp.bfloat16)
    action = jnp.tanh(jnp.dot(policy_normed, w_policy, preferred_element_type=jnp.float32)).astype(
        jnp.bfloat16
    )
    return (imagined, action)


def solution(mesh):
    in_specs = (
        P(("rep", "member", "tp"), None),
        P(("rep", "member", "tp"), None),
        P(("rep", "member", "tp")),
        P(),
        P("member", None, "tp"),
        P("member", "tp", None),
        P(),
        P(),
    )
    out_specs = (P(("rep", "member", "tp"), None), P(("rep", "member", "tp"), None))
    return jax.shard_map(local, mesh=mesh, in_specs=in_specs, out_specs=out_specs, check_vma=False)
```

```python
import jax
import jax.numpy as jnp
from jax import lax
from jax.sharding import PartitionSpec as P

PARTIAL_DTYPE = jnp.bfloat16


def from_partner(value, axis, distance):
    return lax.ppermute(value, axis, [(i, i ^ 1 << distance) for i in range(lax.axis_size(axis))])


def from_chip_behind(value, axis, chips_back):
    size = lax.axis_size(axis)
    return lax.ppermute(value, axis, [(i, (i + 2 * chips_back) % size) for i in range(size)])


def rms_scale(values, gain):
    mean_square = jnp.mean(values * values, axis=-1, keepdims=True)
    return values * lax.rsqrt(mean_square + 1e-06) * gain


def running_rank(member_hits):
    return jnp.sum((jnp.cumsum(member_hits, axis=0) - member_hits) * member_hits, axis=1)


def local(states, member_of, place, norm_gain, w_up, w_down, policy_gain, w_policy):
    n_member = lax.axis_size("member")
    n_tp = lax.axis_size("tp")
    n_dev = n_member * n_tp
    member_total = n_member // 2
    rows_here = states.shape[0]
    feature_width = states.shape[1]
    own_member = lax.axis_index("member") // 2
    own_block = (own_member, w_up[0], w_down[0])
    fetched = [
        (
            (own_member - back + member_total) % member_total,
            from_chip_behind(w_up[0], "member", back),
            from_chip_behind(w_down[0], "member", back),
        )
        for back in range(1, member_total)
    ]
    member = member_of[:, 0]
    gain_rows = jnp.take(norm_gain, member, axis=0)
    normed = rms_scale(states.astype(jnp.float32), gain_rows).astype(jnp.bfloat16)
    member_lanes = jnp.where(
        jnp.arange(128, dtype=jnp.int32)[None, :] == 0, member[:, None], 0
    ).astype(jnp.bfloat16)
    gathered = lax.all_gather(
        jnp.concatenate([normed, member_lanes], axis=1), "tp", axis=0, tiled=True
    )
    gathered_rows = gathered[:, :feature_width]
    gathered_member = gathered[:, feature_width].astype(jnp.int32)

    def apply_block(block_member, up_here, down_here):
        keep = (gathered_member == block_member).astype(jnp.bfloat16)[:, None]
        hidden = jax.nn.gelu(
            jnp.dot(gathered_rows, up_here, preferred_element_type=jnp.float32)
        ).astype(jnp.bfloat16) * keep
        return jnp.dot(hidden, down_here, preferred_element_type=jnp.float32)

    def apply_pair(block_member, up_here, down_here):
        both_up = jnp.concatenate([up_here, from_partner(up_here, "member", 0)], axis=1)
        both_down = jnp.concatenate([down_here, from_partner(down_here, "member", 0)], axis=0)
        return apply_block(block_member, both_up, both_down)

    partial = apply_pair(*own_block)
    for block_member, up_here, down_here in fetched:
        partial, up_here, down_here = lax.optimization_barrier((partial, up_here, down_here))
        partial = partial + apply_pair(block_member, up_here, down_here)
    tp_here = lax.axis_index("tp")
    by_target = partial.reshape(n_tp, rows_here, feature_width)
    change = lax.dynamic_index_in_dim(by_target, tp_here, 0, keepdims=False)
    for shift in range(1, n_tp):
        outgoing = lax.dynamic_index_in_dim(by_target, (tp_here + shift) % n_tp, 0, keepdims=False)
        change = change + lax.ppermute(
            outgoing.astype(PARTIAL_DTYPE),
            "tp",
            [(i, (i + shift) % n_tp) for i in range(n_tp)],
        ).astype(jnp.float32)
    own_rows = (states.astype(jnp.float32) + change).astype(jnp.bfloat16)
    per_learner = rows_here // n_dev
    learner = place // rows_here
    learner_hits = (learner[:, None] == jnp.arange(n_dev, dtype=jnp.int32)[None, :]).astype(
        jnp.int32
    )
    lane_index = learner * per_learner + running_rank(learner_hits)
    placer = jnp.arange(rows_here, dtype=jnp.int32)[:, None] == lane_index[None, :]
    spot_index = place % rows_here
    packed = jnp.dot(
        placer.astype(jnp.bfloat16), own_rows, preferred_element_type=jnp.float32
    ).astype(jnp.bfloat16)
    packed_spot = jnp.sum(placer.astype(jnp.int32) * spot_index[None, :], axis=1)
    spot_lanes = jnp.where(
        jnp.arange(128, dtype=jnp.int32)[None, :] == 0, packed_spot[:, None], 0
    ).astype(jnp.bfloat16)
    arrivals = lax.all_to_all(
        jnp.concatenate([packed, spot_lanes], axis=1).reshape(n_dev, per_learner, feature_width + 128),
        ("member", "tp"),
        split_axis=0,
        concat_axis=0,
        tiled=True,
    )
    arrivals = arrivals.reshape(n_dev * per_learner, feature_width + 128)
    arrival_spots = arrivals[:, feature_width].astype(jnp.int32)
    settle = (jnp.arange(rows_here, dtype=jnp.int32)[:, None] == arrival_spots[None, :]).astype(
        jnp.bfloat16
    )
    imagined = jnp.dot(
        settle, arrivals[:, :feature_width], preferred_element_type=jnp.float32
    ).astype(jnp.bfloat16)
    policy_normed = rms_scale(imagined.astype(jnp.float32), policy_gain).astype(jnp.bfloat16)
    action = jnp.tanh(jnp.dot(policy_normed, w_policy, preferred_element_type=jnp.float32)).astype(
        jnp.bfloat16
    )
    return (imagined, action)


def solution(mesh):
    in_specs = (
        P(("rep", "member", "tp"), None),
        P(("rep", "member", "tp"), None),
        P(("rep", "member", "tp")),
        P(),
        P("member", None, "tp"),
        P("member", "tp", None),
        P(),
        P(),
    )
    out_specs = (P(("rep", "member", "tp"), None), P(("rep", "member", "tp"), None))
    return jax.shard_map(local, mesh=mesh, in_specs=in_specs, out_specs=out_specs, check_vma=False)
```

```python
import jax
import jax.numpy as jnp
from jax import lax
from jax.sharding import PartitionSpec as P

PARTIAL_DTYPE = jnp.bfloat16


def from_partner(value, axis, distance):
    return lax.ppermute(value, axis, [(i, i ^ 1 << distance) for i in range(lax.axis_size(axis))])


def from_chip_behind(value, axis, chips_back):
    size = lax.axis_size(axis)
    return lax.ppermute(value, axis, [(i, (i + 2 * chips_back) % size) for i in range(size)])


def swap_parts(value):
    n_rep = lax.axis_size("rep")
    return [value] + [
        lax.ppermute(value, "rep", [(i, (i + step) % n_rep) for i in range(n_rep)])
        for step in range(1, n_rep)
    ]


def fetch_shared(up, down, chips_back):
    n_rep = lax.axis_size("rep")
    share = up.shape[1] // n_rep
    rep_here = lax.axis_index("rep")
    got_up = from_chip_behind(
        lax.dynamic_slice_in_dim(up, rep_here * share, share, axis=1), "member", chips_back
    )
    got_up, down = lax.optimization_barrier((got_up, down))
    got_down = from_chip_behind(
        lax.dynamic_slice_in_dim(down, rep_here * share, share, axis=0), "member", chips_back
    )
    up_parts = swap_parts(got_up)
    return jnp.concatenate(up_parts, axis=1), jnp.concatenate(swap_parts(got_down), axis=0)


def rms_scale(values, gain):
    mean_square = jnp.mean(values * values, axis=-1, keepdims=True)
    return values * lax.rsqrt(mean_square + 1e-06) * gain


def running_rank(member_hits):
    return jnp.sum((jnp.cumsum(member_hits, axis=0) - member_hits) * member_hits, axis=1)


def local(states, member_of, place, norm_gain, w_up, w_down, policy_gain, w_policy):
    n_member = lax.axis_size("member")
    n_tp = lax.axis_size("tp")
    n_dev = n_member * n_tp
    member_total = n_member // 2
    rows_here = states.shape[0]
    feature_width = states.shape[1]
    own_member = lax.axis_index("member") // 2
    own_block = (own_member, w_up[0], w_down[0])
    fetched = [
        (
            (own_member - back + member_total) % member_total,
            *fetch_shared(w_up[0], w_down[0], back),
        )
        for back in range(1, member_total)
    ]
    member = member_of[:, 0]
    gain_rows = jnp.take(norm_gain, member, axis=0)
    normed = rms_scale(states.astype(jnp.float32), gain_rows).astype(jnp.bfloat16)
    member_lanes = jnp.where(
        jnp.arange(128, dtype=jnp.int32)[None, :] == 0, member[:, None], 0
    ).astype(jnp.bfloat16)
    gathered = lax.all_gather(
        jnp.concatenate([normed, member_lanes], axis=1), "tp", axis=0, tiled=True
    )
    gathered_rows = gathered[:, :feature_width]
    gathered_member = gathered[:, feature_width].astype(jnp.int32)

    def apply_block(block_member, up_here, down_here):
        keep = (gathered_member == block_member).astype(jnp.bfloat16)[:, None]
        hidden = jax.nn.gelu(
            jnp.dot(gathered_rows, up_here, preferred_element_type=jnp.float32)
        ).astype(jnp.bfloat16) * keep
        return jnp.dot(hidden, down_here, preferred_element_type=jnp.float32)

    def apply_pair(block_member, up_here, down_here):
        return apply_block(block_member, up_here, down_here) + apply_block(
            block_member, from_partner(up_here, "member", 0), from_partner(down_here, "member", 0)
        )

    partial = apply_pair(*own_block)
    for block_member, up_here, down_here in fetched:
        partial, up_here, down_here = lax.optimization_barrier((partial, up_here, down_here))
        partial = partial + apply_pair(block_member, up_here, down_here)
    tp_here = lax.axis_index("tp")
    by_target = partial.reshape(n_tp, rows_here, feature_width)
    change = lax.dynamic_index_in_dim(by_target, tp_here, 0, keepdims=False)
    for shift in range(1, n_tp):
        outgoing = lax.dynamic_index_in_dim(by_target, (tp_here + shift) % n_tp, 0, keepdims=False)
        change = change + lax.ppermute(
            outgoing.astype(PARTIAL_DTYPE),
            "tp",
            [(i, (i + shift) % n_tp) for i in range(n_tp)],
        ).astype(jnp.float32)
    own_rows = (states.astype(jnp.float32) + change).astype(jnp.bfloat16)
    per_learner = rows_here // n_dev
    learner = place // rows_here
    learner_hits = (learner[:, None] == jnp.arange(n_dev, dtype=jnp.int32)[None, :]).astype(
        jnp.int32
    )
    lane_index = learner * per_learner + running_rank(learner_hits)
    placer = jnp.arange(rows_here, dtype=jnp.int32)[:, None] == lane_index[None, :]
    spot_index = place % rows_here
    packed = jnp.dot(
        placer.astype(jnp.bfloat16), own_rows, preferred_element_type=jnp.float32
    ).astype(jnp.bfloat16)
    packed_spot = jnp.sum(placer.astype(jnp.int32) * spot_index[None, :], axis=1)
    spot_lanes = jnp.where(
        jnp.arange(128, dtype=jnp.int32)[None, :] == 0, packed_spot[:, None], 0
    ).astype(jnp.bfloat16)
    arrivals = lax.all_to_all(
        jnp.concatenate([packed, spot_lanes], axis=1).reshape(n_dev, per_learner, feature_width + 128),
        ("member", "tp"),
        split_axis=0,
        concat_axis=0,
        tiled=True,
    )
    arrivals = arrivals.reshape(n_dev * per_learner, feature_width + 128)
    arrival_spots = arrivals[:, feature_width].astype(jnp.int32)
    settle = (jnp.arange(rows_here, dtype=jnp.int32)[:, None] == arrival_spots[None, :]).astype(
        jnp.bfloat16
    )
    imagined = jnp.dot(
        settle, arrivals[:, :feature_width], preferred_element_type=jnp.float32
    ).astype(jnp.bfloat16)
    policy_normed = rms_scale(imagined.astype(jnp.float32), policy_gain).astype(jnp.bfloat16)
    action = jnp.tanh(jnp.dot(policy_normed, w_policy, preferred_element_type=jnp.float32)).astype(
        jnp.bfloat16
    )
    return (imagined, action)


def solution(mesh):
    in_specs = (
        P(("rep", "member", "tp"), None),
        P(("rep", "member", "tp"), None),
        P(("rep", "member", "tp")),
        P(),
        P("member", None, "tp"),
        P("member", "tp", None),
        P(),
        P(),
    )
    out_specs = (P(("rep", "member", "tp"), None), P(("rep", "member", "tp"), None))
    return jax.shard_map(local, mesh=mesh, in_specs=in_specs, out_specs=out_specs, check_vma=False)
```

```python
import jax
import jax.numpy as jnp
from jax import lax
from jax.sharding import PartitionSpec as P

PARTIAL_DTYPE = jnp.bfloat16


def from_partner(value, axis, distance):
    return lax.ppermute(value, axis, [(i, i ^ 1 << distance) for i in range(lax.axis_size(axis))])


def from_chip_behind(value, axis, chips_back):
    size = lax.axis_size(axis)
    return lax.ppermute(value, axis, [(i, (i + 2 * chips_back) % size) for i in range(size)])


def swap_parts(value):
    n_rep = lax.axis_size("rep")
    return [value] + [
        lax.ppermute(value, "rep", [(i, (i + step) % n_rep) for i in range(n_rep)])
        for step in range(1, n_rep)
    ]


def fetch_shared(up, down, chips_back):
    n_rep = lax.axis_size("rep")
    share = up.shape[1] // n_rep
    rep_here = lax.axis_index("rep")
    got_up = from_chip_behind(
        lax.dynamic_slice_in_dim(up, rep_here * share, share, axis=1), "member", chips_back
    )
    got_up, down = lax.optimization_barrier((got_up, down))
    got_down = from_chip_behind(
        lax.dynamic_slice_in_dim(down, rep_here * share, share, axis=0), "member", chips_back
    )
    up_parts = swap_parts(got_up)
    return jnp.concatenate(up_parts, axis=1), jnp.concatenate(swap_parts(got_down), axis=0)


def rms_scale(values, gain):
    mean_square = jnp.mean(values * values, axis=-1, keepdims=True)
    return values * lax.rsqrt(mean_square + 1e-06) * gain


def running_rank(member_hits):
    return jnp.sum((jnp.cumsum(member_hits, axis=0) - member_hits) * member_hits, axis=1)


def local(states, member_of, place, norm_gain, w_up, w_down, policy_gain, w_policy):
    n_member = lax.axis_size("member")
    n_tp = lax.axis_size("tp")
    n_dev = n_member * n_tp
    member_total = n_member // 2
    rows_here = states.shape[0]
    feature_width = states.shape[1]
    own_member = lax.axis_index("member") // 2
    own_block = (own_member, w_up[0], w_down[0])
    fetched = [
        (
            (own_member - back + member_total) % member_total,
            *fetch_shared(w_up[0], w_down[0], back),
        )
        for back in range(1, member_total)
    ]
    member = member_of[:, 0]
    gain_rows = jnp.take(norm_gain, member, axis=0)
    normed = rms_scale(states.astype(jnp.float32), gain_rows).astype(jnp.bfloat16)
    member_lanes = jnp.where(
        jnp.arange(128, dtype=jnp.int32)[None, :] == 0, member[:, None], 0
    ).astype(jnp.bfloat16)
    gathered = lax.all_gather(
        jnp.concatenate([normed, member_lanes], axis=1), "tp", axis=0, tiled=True
    )
    gathered_rows = gathered[:, :feature_width]
    gathered_member = gathered[:, feature_width].astype(jnp.int32)

    ups, downs, keeps = [], [], []
    for block_member, up_here, down_here in [own_block] + fetched:
        keep = (gathered_member == block_member).astype(jnp.bfloat16)[:, None]
        ups += [up_here, from_partner(up_here, "member", 0)]
        downs += [down_here, from_partner(down_here, "member", 0)]
        keeps += [jnp.broadcast_to(keep, (keep.shape[0], 2 * up_here.shape[1]))]
    hidden = jax.nn.gelu(
        jnp.dot(gathered_rows, jnp.concatenate(ups, axis=1), preferred_element_type=jnp.float32)
    ).astype(jnp.bfloat16) * jnp.concatenate(keeps, axis=1)
    partial = jnp.dot(hidden, jnp.concatenate(downs, axis=0), preferred_element_type=jnp.float32)
    tp_here = lax.axis_index("tp")
    by_target = partial.reshape(n_tp, rows_here, feature_width)
    change = lax.dynamic_index_in_dim(by_target, tp_here, 0, keepdims=False)
    for shift in range(1, n_tp):
        outgoing = lax.dynamic_index_in_dim(by_target, (tp_here + shift) % n_tp, 0, keepdims=False)
        change = change + lax.ppermute(
            outgoing.astype(PARTIAL_DTYPE),
            "tp",
            [(i, (i + shift) % n_tp) for i in range(n_tp)],
        ).astype(jnp.float32)
    own_rows = (states.astype(jnp.float32) + change).astype(jnp.bfloat16)
    per_learner = rows_here // n_dev
    learner = place // rows_here
    learner_hits = (learner[:, None] == jnp.arange(n_dev, dtype=jnp.int32)[None, :]).astype(
        jnp.int32
    )
    lane_index = learner * per_learner + running_rank(learner_hits)
    placer = jnp.arange(rows_here, dtype=jnp.int32)[:, None] == lane_index[None, :]
    spot_index = place % rows_here
    packed = jnp.dot(
        placer.astype(jnp.bfloat16), own_rows, preferred_element_type=jnp.float32
    ).astype(jnp.bfloat16)
    packed_spot = jnp.sum(placer.astype(jnp.int32) * spot_index[None, :], axis=1)
    spot_lanes = jnp.where(
        jnp.arange(128, dtype=jnp.int32)[None, :] == 0, packed_spot[:, None], 0
    ).astype(jnp.bfloat16)
    arrivals = lax.all_to_all(
        jnp.concatenate([packed, spot_lanes], axis=1).reshape(n_dev, per_learner, feature_width + 128),
        ("member", "tp"),
        split_axis=0,
        concat_axis=0,
        tiled=True,
    )
    arrivals = arrivals.reshape(n_dev * per_learner, feature_width + 128)
    arrival_spots = arrivals[:, feature_width].astype(jnp.int32)
    settle = (jnp.arange(rows_here, dtype=jnp.int32)[:, None] == arrival_spots[None, :]).astype(
        jnp.bfloat16
    )
    imagined = jnp.dot(
        settle, arrivals[:, :feature_width], preferred_element_type=jnp.float32
    ).astype(jnp.bfloat16)
    policy_normed = rms_scale(imagined.astype(jnp.float32), policy_gain).astype(jnp.bfloat16)
    action = jnp.tanh(jnp.dot(policy_normed, w_policy, preferred_element_type=jnp.float32)).astype(
        jnp.bfloat16
    )
    return (imagined, action)


def solution(mesh):
    in_specs = (
        P(("rep", "member", "tp"), None),
        P(("rep", "member", "tp"), None),
        P(("rep", "member", "tp")),
        P(),
        P("member", None, "tp"),
        P("member", "tp", None),
        P(),
        P(),
    )
    out_specs = (P(("rep", "member", "tp"), None), P(("rep", "member", "tp"), None))
    return jax.shard_map(local, mesh=mesh, in_specs=in_specs, out_specs=out_specs, check_vma=False)
```

```python
import jax
import jax.numpy as jnp
from jax import lax
from jax.sharding import PartitionSpec as P

PARTIAL_DTYPE = jnp.bfloat16


def from_partner(value, axis, distance):
    return lax.ppermute(value, axis, [(i, i ^ 1 << distance) for i in range(lax.axis_size(axis))])


def from_chip_behind(value, axis, chips_back):
    size = lax.axis_size(axis)
    return lax.ppermute(value, axis, [(i, (i + 2 * chips_back) % size) for i in range(size)])


def swap_parts(value):
    n_rep = lax.axis_size("rep")
    return [value] + [
        lax.ppermute(value, "rep", [(i, (i + step) % n_rep) for i in range(n_rep)])
        for step in range(1, n_rep)
    ]


def fetch_shared(up, down, chips_back):
    n_rep = lax.axis_size("rep")
    share = up.shape[1] // n_rep
    rep_here = lax.axis_index("rep")
    got_up = from_chip_behind(
        lax.dynamic_slice_in_dim(up, rep_here * share, share, axis=1), "member", chips_back
    )
    got_up, down = lax.optimization_barrier((got_up, down))
    got_down = from_chip_behind(
        lax.dynamic_slice_in_dim(down, rep_here * share, share, axis=0), "member", chips_back
    )
    up_parts = swap_parts(got_up)
    return jnp.concatenate(up_parts, axis=1), jnp.concatenate(swap_parts(got_down), axis=0)


def rms_scale(values, gain):
    mean_square = jnp.mean(values * values, axis=-1, keepdims=True)
    return values * lax.rsqrt(mean_square + 1e-06) * gain


def running_rank(member_hits):
    return jnp.sum((jnp.cumsum(member_hits, axis=0) - member_hits) * member_hits, axis=1)


def local(states, member_of, place, norm_gain, w_up, w_down, policy_gain, w_policy):
    n_member = lax.axis_size("member")
    n_tp = lax.axis_size("tp")
    n_dev = n_member * n_tp
    member_total = n_member // 2
    rows_here = states.shape[0]
    feature_width = states.shape[1]
    own_member = lax.axis_index("member") // 2
    own_block = (own_member, w_up[0], w_down[0])
    fetched = [
        (
            (own_member - back + member_total) % member_total,
            *fetch_shared(w_up[0], w_down[0], back),
        )
        for back in range(1, member_total)
    ]
    member = member_of[:, 0]
    gain_rows = jnp.take(norm_gain, member, axis=0)
    normed = rms_scale(states.astype(jnp.float32), gain_rows).astype(jnp.bfloat16)
    member_lanes = jnp.where(
        jnp.arange(128, dtype=jnp.int32)[None, :] == 0, member[:, None], 0
    ).astype(jnp.bfloat16)
    gathered = lax.all_gather(
        jnp.concatenate([normed, member_lanes], axis=1), "tp", axis=0, tiled=True
    )
    gathered_rows = gathered[:, :feature_width]
    gathered_member = gathered[:, feature_width].astype(jnp.int32)

    def apply_block(block_member, up_here, down_here):
        keep = (gathered_member == block_member).astype(jnp.bfloat16)[:, None]
        hidden = jax.nn.gelu(
            jnp.dot(gathered_rows, up_here, preferred_element_type=jnp.float32)
        ).astype(jnp.bfloat16) * keep
        return jnp.dot(hidden, down_here, preferred_element_type=jnp.float32)

    def apply_pair(block_member, up_here, down_here):
        both_up = jnp.concatenate([up_here, from_partner(up_here, "member", 0)], axis=1)
        both_down = jnp.concatenate([down_here, from_partner(down_here, "member", 0)], axis=0)
        return apply_block(block_member, both_up, both_down)

    partial = apply_pair(*own_block)
    for block_member, up_here, down_here in fetched:
        partial, up_here, down_here = lax.optimization_barrier((partial, up_here, down_here))
        partial = partial + apply_pair(block_member, up_here, down_here)
    tp_here = lax.axis_index("tp")
    by_target = partial.reshape(n_tp, rows_here, feature_width)
    change = lax.dynamic_index_in_dim(by_target, tp_here, 0, keepdims=False)
    for shift in range(1, n_tp):
        outgoing = lax.dynamic_index_in_dim(by_target, (tp_here + shift) % n_tp, 0, keepdims=False)
        change = change + lax.ppermute(
            outgoing.astype(PARTIAL_DTYPE),
            "tp",
            [(i, (i + shift) % n_tp) for i in range(n_tp)],
        ).astype(jnp.float32)
    own_rows = (states.astype(jnp.float32) + change).astype(jnp.bfloat16)
    per_learner = rows_here // n_dev
    learner = place // rows_here
    learner_hits = (learner[:, None] == jnp.arange(n_dev, dtype=jnp.int32)[None, :]).astype(
        jnp.int32
    )
    lane_index = learner * per_learner + running_rank(learner_hits)
    placer = jnp.arange(rows_here, dtype=jnp.int32)[:, None] == lane_index[None, :]
    spot_index = place % rows_here
    packed = jnp.dot(
        placer.astype(jnp.bfloat16), own_rows, preferred_element_type=jnp.float32
    ).astype(jnp.bfloat16)
    packed_spot = jnp.sum(placer.astype(jnp.int32) * spot_index[None, :], axis=1)
    spot_lanes = jnp.where(
        jnp.arange(128, dtype=jnp.int32)[None, :] == 0, packed_spot[:, None], 0
    ).astype(jnp.bfloat16)
    arrivals = lax.all_to_all(
        jnp.concatenate([packed, spot_lanes], axis=1).reshape(n_dev, per_learner, feature_width + 128),
        ("member", "tp"),
        split_axis=0,
        concat_axis=0,
        tiled=True,
    )
    arrivals = arrivals.reshape(n_dev * per_learner, feature_width + 128)
    arrival_spots = arrivals[:, feature_width].astype(jnp.int32)
    settle = (jnp.arange(rows_here, dtype=jnp.int32)[:, None] == arrival_spots[None, :]).astype(
        jnp.bfloat16
    )
    imagined = jnp.dot(
        settle, arrivals[:, :feature_width], preferred_element_type=jnp.float32
    ).astype(jnp.bfloat16)
    policy_normed = rms_scale(imagined.astype(jnp.float32), policy_gain).astype(jnp.bfloat16)
    action = jnp.tanh(jnp.dot(policy_normed, w_policy, preferred_element_type=jnp.float32)).astype(
        jnp.bfloat16
    )
    return (imagined, action)


def solution(mesh):
    in_specs = (
        P(("rep", "member", "tp"), None),
        P(("rep", "member", "tp"), None),
        P(("rep", "member", "tp")),
        P(),
        P("member", None, "tp"),
        P("member", "tp", None),
        P(),
        P(),
    )
    out_specs = (P(("rep", "member", "tp"), None), P(("rep", "member", "tp"), None))
    return jax.shard_map(local, mesh=mesh, in_specs=in_specs, out_specs=out_specs, check_vma=False)
```

```python
import jax
import jax.numpy as jnp
from jax import lax
from jax.sharding import PartitionSpec as P

PARTIAL_DTYPE = jnp.bfloat16


def from_partner(value, axis, distance):
    return lax.ppermute(value, axis, [(i, i ^ 1 << distance) for i in range(lax.axis_size(axis))])


def from_chip_behind(value, axis, chips_back):
    size = lax.axis_size(axis)
    return lax.ppermute(value, axis, [(i, (i + 2 * chips_back) % size) for i in range(size)])


def swap_parts(value):
    n_rep = lax.axis_size("rep")
    return [value] + [
        lax.ppermute(value, "rep", [(i, (i + step) % n_rep) for i in range(n_rep)])
        for step in range(1, n_rep)
    ]


def fetch_shared(up, down, chips_back):
    n_rep = lax.axis_size("rep")
    share = up.shape[1] // n_rep
    rep_here = lax.axis_index("rep")
    got_up = from_chip_behind(
        lax.dynamic_slice_in_dim(up, rep_here * share, share, axis=1), "member", chips_back
    )
    got_up, down = lax.optimization_barrier((got_up, down))
    got_down = from_chip_behind(
        lax.dynamic_slice_in_dim(down, rep_here * share, share, axis=0), "member", chips_back
    )
    up_parts = swap_parts(got_up)
    return jnp.concatenate(up_parts, axis=1), jnp.concatenate(swap_parts(got_down), axis=0)


def rms_scale(values, gain):
    mean_square = jnp.mean(values * values, axis=-1, keepdims=True)
    return values * lax.rsqrt(mean_square + 1e-06) * gain


def running_rank(member_hits):
    return jnp.sum((jnp.cumsum(member_hits, axis=0) - member_hits) * member_hits, axis=1)


def local(states, member_of, place, norm_gain, w_up, w_down, policy_gain, w_policy):
    n_member = lax.axis_size("member")
    n_tp = lax.axis_size("tp")
    n_dev = n_member * n_tp
    member_total = n_member // 2
    rows_here = states.shape[0]
    feature_width = states.shape[1]
    own_member = lax.axis_index("member") // 2
    own_block = (own_member, w_up[0], w_down[0])
    fetched = [
        (
            (own_member - back + member_total) % member_total,
            *fetch_shared(w_up[0], w_down[0], back),
        )
        for back in range(1, member_total)
    ]
    member = member_of[:, 0]
    gain_rows = jnp.take(norm_gain, member, axis=0)
    normed = rms_scale(states.astype(jnp.float32), gain_rows).astype(jnp.bfloat16)
    member_lanes = jnp.where(
        jnp.arange(128, dtype=jnp.int32)[None, :] == 0, member[:, None], 0
    ).astype(jnp.bfloat16)
    gathered = lax.all_gather(
        jnp.concatenate([normed, member_lanes], axis=1), "tp", axis=0, tiled=True
    )
    gathered_rows = gathered[:, :feature_width]
    gathered_member = gathered[:, feature_width].astype(jnp.int32)

    def apply_block(block_member, up_here, down_here):
        keep = (gathered_member == block_member).astype(jnp.bfloat16)[:, None]
        hidden = jax.nn.gelu(
            jnp.dot(gathered_rows, up_here, preferred_element_type=jnp.float32)
        ).astype(jnp.bfloat16) * keep
        return jnp.dot(hidden, down_here, preferred_element_type=jnp.float32)

    def apply_pair(block_member, up_here, down_here):
        both_up = jnp.concatenate([up_here, from_partner(up_here, "member", 0)], axis=1)
        both_down = jnp.concatenate([down_here, from_partner(down_here, "member", 0)], axis=0)
        return apply_block(block_member, both_up, both_down)

    terms = [apply_pair(*own_block)]
    for block_member, up_here, down_here in fetched:
        terms, up_here, down_here = lax.optimization_barrier((terms, up_here, down_here))
        terms = terms + [apply_pair(block_member, up_here, down_here)]
    tp_here = lax.axis_index("tp")
    by_target = [term.reshape(n_tp, rows_here, feature_width) for term in terms]

    def slice_for(target):
        pieces = [lax.dynamic_index_in_dim(term, target, 0, keepdims=False) for term in by_target]
        total = pieces[0]
        for piece in pieces[1:]:
            total = total + piece
        return total

    change = slice_for(tp_here)
    for shift in range(1, n_tp):
        change = change + lax.ppermute(
            slice_for((tp_here + shift) % n_tp).astype(PARTIAL_DTYPE),
            "tp",
            [(i, (i + shift) % n_tp) for i in range(n_tp)],
        ).astype(jnp.float32)
    own_rows = (states.astype(jnp.float32) + change).astype(jnp.bfloat16)
    per_learner = rows_here // n_dev
    learner = place // rows_here
    learner_hits = (learner[:, None] == jnp.arange(n_dev, dtype=jnp.int32)[None, :]).astype(
        jnp.int32
    )
    lane_index = learner * per_learner + running_rank(learner_hits)
    placer = jnp.arange(rows_here, dtype=jnp.int32)[:, None] == lane_index[None, :]
    spot_index = place % rows_here
    packed = jnp.dot(
        placer.astype(jnp.bfloat16), own_rows, preferred_element_type=jnp.float32
    ).astype(jnp.bfloat16)
    packed_spot = jnp.sum(placer.astype(jnp.int32) * spot_index[None, :], axis=1)
    spot_lanes = jnp.where(
        jnp.arange(128, dtype=jnp.int32)[None, :] == 0, packed_spot[:, None], 0
    ).astype(jnp.bfloat16)
    arrivals = lax.all_to_all(
        jnp.concatenate([packed, spot_lanes], axis=1).reshape(n_dev, per_learner, feature_width + 128),
        ("member", "tp"),
        split_axis=0,
        concat_axis=0,
        tiled=True,
    )
    arrivals = arrivals.reshape(n_dev * per_learner, feature_width + 128)
    arrival_spots = arrivals[:, feature_width].astype(jnp.int32)
    settle = (jnp.arange(rows_here, dtype=jnp.int32)[:, None] == arrival_spots[None, :]).astype(
        jnp.bfloat16
    )
    imagined = jnp.dot(
        settle, arrivals[:, :feature_width], preferred_element_type=jnp.float32
    ).astype(jnp.bfloat16)
    policy_normed = rms_scale(imagined.astype(jnp.float32), policy_gain).astype(jnp.bfloat16)
    action = jnp.tanh(jnp.dot(policy_normed, w_policy, preferred_element_type=jnp.float32)).astype(
        jnp.bfloat16
    )
    return (imagined, action)


def solution(mesh):
    in_specs = (
        P(("rep", "member", "tp"), None),
        P(("rep", "member", "tp"), None),
        P(("rep", "member", "tp")),
        P(),
        P("member", None, "tp"),
        P("member", "tp", None),
        P(),
        P(),
    )
    out_specs = (P(("rep", "member", "tp"), None), P(("rep", "member", "tp"), None))
    return jax.shard_map(local, mesh=mesh, in_specs=in_specs, out_specs=out_specs, check_vma=False)
```

```python
import jax
import jax.numpy as jnp
from jax import lax
from jax.sharding import PartitionSpec as P

PARTIAL_DTYPE = jnp.bfloat16


def from_partner(value, axis, distance):
    return lax.ppermute(value, axis, [(i, i ^ 1 << distance) for i in range(lax.axis_size(axis))])


def from_chip_behind(value, axis, chips_back):
    size = lax.axis_size(axis)
    return lax.ppermute(value, axis, [(i, (i + 2 * chips_back) % size) for i in range(size)])


def swap_parts(value):
    n_rep = lax.axis_size("rep")
    return [value] + [
        lax.ppermute(value, "rep", [(i, (i + step) % n_rep) for i in range(n_rep)])
        for step in range(1, n_rep)
    ]


def fetch_shared(up, down, chips_back):
    n_rep = lax.axis_size("rep")
    share = up.shape[1] // n_rep
    rep_here = lax.axis_index("rep")
    got_up = from_chip_behind(
        lax.dynamic_slice_in_dim(up, rep_here * share, share, axis=1), "member", chips_back
    )
    got_up, down = lax.optimization_barrier((got_up, down))
    got_down = from_chip_behind(
        lax.dynamic_slice_in_dim(down, rep_here * share, share, axis=0), "member", chips_back
    )
    up_parts = swap_parts(got_up)
    return jnp.concatenate(up_parts, axis=1), jnp.concatenate(swap_parts(got_down), axis=0)


def rms_scale(values, gain):
    mean_square = jnp.mean(values * values, axis=-1, keepdims=True)
    return values * lax.rsqrt(mean_square + 1e-06) * gain


def running_rank(member_hits):
    return jnp.sum((jnp.cumsum(member_hits, axis=0) - member_hits) * member_hits, axis=1)


def local(states, member_of, place, norm_gain, w_up, w_down, policy_gain, w_policy):
    n_member = lax.axis_size("member")
    n_tp = lax.axis_size("tp")
    n_dev = n_member * n_tp
    member_total = n_member // 2
    rows_here = states.shape[0]
    feature_width = states.shape[1]
    own_member = lax.axis_index("member") // 2
    own_block = (own_member, w_up[0], w_down[0])
    fetched = [
        (
            (own_member - back + member_total) % member_total,
            *fetch_shared(w_up[0], w_down[0], back),
        )
        for back in range(1, member_total)
    ]
    member = member_of[:, 0]
    gain_rows = jnp.take(norm_gain, member, axis=0)
    normed = rms_scale(states.astype(jnp.float32), gain_rows).astype(jnp.bfloat16)
    member_lanes = jnp.where(
        jnp.arange(128, dtype=jnp.int32)[None, :] == 0, member[:, None], 0
    ).astype(jnp.bfloat16)
    gathered = lax.all_gather(
        jnp.concatenate([normed, member_lanes], axis=1), "tp", axis=0, tiled=True
    )
    tp_here = lax.axis_index("tp")
    by_source = gathered.reshape(n_tp, rows_here, feature_width + 128)
    shifts = list(range(1, n_tp)) + [0]
    row_blocks = [
        lax.dynamic_index_in_dim(by_source, (tp_here + shift) % n_tp, 0, keepdims=False)
        for shift in shifts
    ]

    def apply_block(rows_block, block_member, up_here, down_here):
        keep = (rows_block[:, feature_width].astype(jnp.int32) == block_member).astype(jnp.bfloat16)
        hidden = jax.nn.gelu(
            jnp.dot(rows_block[:, :feature_width], up_here, preferred_element_type=jnp.float32)
        ).astype(jnp.bfloat16) * keep[:, None]
        return jnp.dot(hidden, down_here, preferred_element_type=jnp.float32)

    def both_halves(block_member, up_here, down_here):
        both_up = jnp.concatenate([up_here, from_partner(up_here, "member", 0)], axis=1)
        both_down = jnp.concatenate([down_here, from_partner(down_here, "member", 0)], axis=0)
        return block_member, both_up, both_down

    own_pair = both_halves(*own_block)
    totals = [apply_block(rows_block, *own_pair) for rows_block in row_blocks]
    for block_member, up_here, down_here in fetched:
        totals, up_here, down_here = lax.optimization_barrier((totals, up_here, down_here))
        pair = both_halves(block_member, up_here, down_here)
        totals = [total + apply_block(rows_block, *pair) for total, rows_block in zip(totals, row_blocks)]
    change = totals[-1]
    for shift, total in zip(shifts[:-1], totals[:-1]):
        change = change + lax.ppermute(
            total.astype(PARTIAL_DTYPE),
            "tp",
            [(i, (i + shift) % n_tp) for i in range(n_tp)],
        ).astype(jnp.float32)
    own_rows = (states.astype(jnp.float32) + change).astype(jnp.bfloat16)
    per_learner = rows_here // n_dev
    learner = place // rows_here
    learner_hits = (learner[:, None] == jnp.arange(n_dev, dtype=jnp.int32)[None, :]).astype(
        jnp.int32
    )
    lane_index = learner * per_learner + running_rank(learner_hits)
    placer = jnp.arange(rows_here, dtype=jnp.int32)[:, None] == lane_index[None, :]
    spot_index = place % rows_here
    packed = jnp.dot(
        placer.astype(jnp.bfloat16), own_rows, preferred_element_type=jnp.float32
    ).astype(jnp.bfloat16)
    packed_spot = jnp.sum(placer.astype(jnp.int32) * spot_index[None, :], axis=1)
    spot_lanes = jnp.where(
        jnp.arange(128, dtype=jnp.int32)[None, :] == 0, packed_spot[:, None], 0
    ).astype(jnp.bfloat16)
    arrivals = lax.all_to_all(
        jnp.concatenate([packed, spot_lanes], axis=1).reshape(n_dev, per_learner, feature_width + 128),
        ("member", "tp"),
        split_axis=0,
        concat_axis=0,
        tiled=True,
    )
    arrivals = arrivals.reshape(n_dev * per_learner, feature_width + 128)
    arrival_spots = arrivals[:, feature_width].astype(jnp.int32)
    settle = (jnp.arange(rows_here, dtype=jnp.int32)[:, None] == arrival_spots[None, :]).astype(
        jnp.bfloat16
    )
    imagined = jnp.dot(
        settle, arrivals[:, :feature_width], preferred_element_type=jnp.float32
    ).astype(jnp.bfloat16)
    policy_normed = rms_scale(imagined.astype(jnp.float32), policy_gain).astype(jnp.bfloat16)
    action = jnp.tanh(jnp.dot(policy_normed, w_policy, preferred_element_type=jnp.float32)).astype(
        jnp.bfloat16
    )
    return (imagined, action)


def solution(mesh):
    in_specs = (
        P(("rep", "member", "tp"), None),
        P(("rep", "member", "tp"), None),
        P(("rep", "member", "tp")),
        P(),
        P("member", None, "tp"),
        P("member", "tp", None),
        P(),
        P(),
    )
    out_specs = (P(("rep", "member", "tp"), None), P(("rep", "member", "tp"), None))
    return jax.shard_map(local, mesh=mesh, in_specs=in_specs, out_specs=out_specs, check_vma=False)
```

```python
import jax
import jax.numpy as jnp
from jax import lax
from jax.sharding import PartitionSpec as P

PARTIAL_DTYPE = jnp.bfloat16


def from_partner(value, axis, distance):
    return lax.ppermute(value, axis, [(i, i ^ 1 << distance) for i in range(lax.axis_size(axis))])


def from_chip_behind(value, axis, chips_back):
    size = lax.axis_size(axis)
    return lax.ppermute(value, axis, [(i, (i + 2 * chips_back) % size) for i in range(size)])


def swap_parts(value):
    n_rep = lax.axis_size("rep")
    return [value] + [
        lax.ppermute(value, "rep", [(i, (i + step) % n_rep) for i in range(n_rep)])
        for step in range(1, n_rep)
    ]


def fetch_shared(up, down, chips_back):
    n_rep = lax.axis_size("rep")
    share = up.shape[1] // n_rep
    rep_here = lax.axis_index("rep")
    got_up = from_chip_behind(
        lax.dynamic_slice_in_dim(up, rep_here * share, share, axis=1), "member", chips_back
    )
    got_up, down = lax.optimization_barrier((got_up, down))
    got_down = from_chip_behind(
        lax.dynamic_slice_in_dim(down, rep_here * share, share, axis=0), "member", chips_back
    )
    up_parts = swap_parts(got_up)
    down_parts = swap_parts(got_down)
    partner_up = [from_partner(part, "member", 0) for part in up_parts]
    partner_down = [from_partner(part, "member", 0) for part in down_parts]
    return (
        jnp.concatenate(up_parts + partner_up, axis=1),
        jnp.concatenate(down_parts + partner_down, axis=0),
    )


def rms_scale(values, gain):
    mean_square = jnp.mean(values * values, axis=-1, keepdims=True)
    return values * lax.rsqrt(mean_square + 1e-06) * gain


def running_rank(member_hits):
    return jnp.sum((jnp.cumsum(member_hits, axis=0) - member_hits) * member_hits, axis=1)


def local(states, member_of, place, norm_gain, w_up, w_down, policy_gain, w_policy):
    n_member = lax.axis_size("member")
    n_tp = lax.axis_size("tp")
    n_dev = n_member * n_tp
    member_total = n_member // 2
    rows_here = states.shape[0]
    feature_width = states.shape[1]
    own_member = lax.axis_index("member") // 2
    own_block = (own_member, w_up[0], w_down[0])
    fetched = [
        (
            (own_member - back + member_total) % member_total,
            *fetch_shared(w_up[0], w_down[0], back),
        )
        for back in range(1, member_total)
    ]
    member = member_of[:, 0]
    gain_rows = jnp.take(norm_gain, member, axis=0)
    normed = rms_scale(states.astype(jnp.float32), gain_rows).astype(jnp.bfloat16)
    member_lanes = jnp.where(
        jnp.arange(128, dtype=jnp.int32)[None, :] == 0, member[:, None], 0
    ).astype(jnp.bfloat16)
    gathered = lax.all_gather(
        jnp.concatenate([normed, member_lanes], axis=1), "tp", axis=0, tiled=True
    )
    gathered_rows = gathered[:, :feature_width]
    gathered_member = gathered[:, feature_width].astype(jnp.int32)

    def apply_block(block_member, up_here, down_here):
        keep = (gathered_member == block_member).astype(jnp.bfloat16)[:, None]
        hidden = jax.nn.gelu(
            jnp.dot(gathered_rows, up_here, preferred_element_type=jnp.float32)
        ).astype(jnp.bfloat16) * keep
        return jnp.dot(hidden, down_here, preferred_element_type=jnp.float32)

    def apply_pair(block_member, up_here, down_here):
        both_up = jnp.concatenate([up_here, from_partner(up_here, "member", 0)], axis=1)
        both_down = jnp.concatenate([down_here, from_partner(down_here, "member", 0)], axis=0)
        return apply_block(block_member, both_up, both_down)

    terms = [apply_pair(*own_block)]
    for block_member, up_here, down_here in fetched:
        terms, up_here, down_here = lax.optimization_barrier((terms, up_here, down_here))
        terms = terms + [apply_block(block_member, up_here, down_here)]
    tp_here = lax.axis_index("tp")
    by_target = [term.reshape(n_tp, rows_here, feature_width) for term in terms]

    def slice_for(target):
        pieces = [lax.dynamic_index_in_dim(term, target, 0, keepdims=False) for term in by_target]
        total = pieces[0]
        for piece in pieces[1:]:
            total = total + piece
        return total

    change = slice_for(tp_here)
    for shift in range(1, n_tp):
        change = change + lax.ppermute(
            slice_for((tp_here + shift) % n_tp).astype(PARTIAL_DTYPE),
            "tp",
            [(i, (i + shift) % n_tp) for i in range(n_tp)],
        ).astype(jnp.float32)
    own_rows = (states.astype(jnp.float32) + change).astype(jnp.bfloat16)
    per_learner = rows_here // n_dev
    learner = place // rows_here
    learner_hits = (learner[:, None] == jnp.arange(n_dev, dtype=jnp.int32)[None, :]).astype(
        jnp.int32
    )
    lane_index = learner * per_learner + running_rank(learner_hits)
    placer = jnp.arange(rows_here, dtype=jnp.int32)[:, None] == lane_index[None, :]
    spot_index = place % rows_here
    packed = jnp.dot(
        placer.astype(jnp.bfloat16), own_rows, preferred_element_type=jnp.float32
    ).astype(jnp.bfloat16)
    packed_spot = jnp.sum(placer.astype(jnp.int32) * spot_index[None, :], axis=1)
    spot_lanes = jnp.where(
        jnp.arange(128, dtype=jnp.int32)[None, :] == 0, packed_spot[:, None], 0
    ).astype(jnp.bfloat16)
    arrivals = lax.all_to_all(
        jnp.concatenate([packed, spot_lanes], axis=1).reshape(n_dev, per_learner, feature_width + 128),
        ("member", "tp"),
        split_axis=0,
        concat_axis=0,
        tiled=True,
    )
    arrivals = arrivals.reshape(n_dev * per_learner, feature_width + 128)
    arrival_spots = arrivals[:, feature_width].astype(jnp.int32)
    settle = (jnp.arange(rows_here, dtype=jnp.int32)[:, None] == arrival_spots[None, :]).astype(
        jnp.bfloat16
    )
    imagined = jnp.dot(
        settle, arrivals[:, :feature_width], preferred_element_type=jnp.float32
    ).astype(jnp.bfloat16)
    policy_normed = rms_scale(imagined.astype(jnp.float32), policy_gain).astype(jnp.bfloat16)
    action = jnp.tanh(jnp.dot(policy_normed, w_policy, preferred_element_type=jnp.float32)).astype(
        jnp.bfloat16
    )
    return (imagined, action)


def solution(mesh):
    in_specs = (
        P(("rep", "member", "tp"), None),
        P(("rep", "member", "tp"), None),
        P(("rep", "member", "tp")),
        P(),
        P("member", None, "tp"),
        P("member", "tp", None),
        P(),
        P(),
    )
    out_specs = (P(("rep", "member", "tp"), None), P(("rep", "member", "tp"), None))
    return jax.shard_map(local, mesh=mesh, in_specs=in_specs, out_specs=out_specs, check_vma=False)
```

```python
import jax
import jax.numpy as jnp
from jax import lax
from jax.sharding import PartitionSpec as P

PARTIAL_DTYPE = jnp.bfloat16


def from_partner(value, axis, distance):
    return lax.ppermute(value, axis, [(i, i ^ 1 << distance) for i in range(lax.axis_size(axis))])


def from_chip_behind(value, axis, chips_back):
    size = lax.axis_size(axis)
    return lax.ppermute(value, axis, [(i, (i + 2 * chips_back) % size) for i in range(size)])


def swap_parts(value):
    n_rep = lax.axis_size("rep")
    return [value] + [
        lax.ppermute(value, "rep", [(i, (i + step) % n_rep) for i in range(n_rep)])
        for step in range(1, n_rep)
    ]


def fetch_shared(up, down, chips_back):
    n_rep = lax.axis_size("rep")
    share = up.shape[1] // n_rep
    rep_here = lax.axis_index("rep")
    got_up = from_chip_behind(
        lax.dynamic_slice_in_dim(up, rep_here * share, share, axis=1), "member", chips_back
    )
    got_up, down = lax.optimization_barrier((got_up, down))
    got_down = from_chip_behind(
        lax.dynamic_slice_in_dim(down, rep_here * share, share, axis=0), "member", chips_back
    )
    up_parts = swap_parts(got_up)
    down_parts = swap_parts(got_down)
    partner_up = [from_partner(part, "member", 0) for part in up_parts]
    partner_down = [from_partner(part, "member", 0) for part in down_parts]
    return (
        jnp.concatenate(up_parts + partner_up, axis=1),
        jnp.concatenate(down_parts + partner_down, axis=0),
    )


def rms_scale(values, gain):
    mean_square = jnp.mean(values * values, axis=-1, keepdims=True)
    return values * lax.rsqrt(mean_square + 1e-06) * gain


def running_rank(member_hits):
    return jnp.sum((jnp.cumsum(member_hits, axis=0) - member_hits) * member_hits, axis=1)


def local(states, member_of, place, norm_gain, w_up, w_down, policy_gain, w_policy):
    n_member = lax.axis_size("member")
    n_tp = lax.axis_size("tp")
    n_dev = n_member * n_tp
    member_total = n_member // 2
    rows_here = states.shape[0]
    feature_width = states.shape[1]
    own_member = lax.axis_index("member") // 2
    own_block = (own_member, w_up[0], w_down[0])
    fetched = [
        (
            (own_member - back + member_total) % member_total,
            *fetch_shared(w_up[0], w_down[0], back),
        )
        for back in range(1, member_total)
    ]
    member = member_of[:, 0]
    gain_rows = jnp.take(norm_gain, member, axis=0)
    normed = rms_scale(states.astype(jnp.float32), gain_rows).astype(jnp.bfloat16)
    member_lanes = jnp.where(
        jnp.arange(128, dtype=jnp.int32)[None, :] == 0, member[:, None], 0
    ).astype(jnp.bfloat16)
    gathered = lax.all_gather(
        jnp.concatenate([normed, member_lanes], axis=1), "tp", axis=0, tiled=True
    )
    gathered_rows = gathered[:, :feature_width]
    gathered_member = gathered[:, feature_width].astype(jnp.int32)

    def apply_block(block_member, up_here, down_here):
        keep = (gathered_member == block_member).astype(jnp.bfloat16)[:, None]
        hidden = jax.nn.gelu(
            jnp.dot(gathered_rows, up_here, preferred_element_type=jnp.float32)
        ).astype(jnp.bfloat16) * keep
        return jnp.dot(hidden, down_here, preferred_element_type=jnp.float32)

    def apply_pair(block_member, up_here, down_here):
        both_up = jnp.concatenate([up_here, from_partner(up_here, "member", 0)], axis=1)
        both_down = jnp.concatenate([down_here, from_partner(down_here, "member", 0)], axis=0)
        return apply_block(block_member, both_up, both_down)

    terms = [apply_pair(*own_block)]
    for block_member, up_here, down_here in fetched:
        terms, up_here, down_here = lax.optimization_barrier((terms, up_here, down_here))
        terms = terms + [apply_block(block_member, up_here, down_here)]
    total = terms[0]
    for term in terms[1:]:
        total = total + term
    change = lax.psum_scatter(
        total.astype(PARTIAL_DTYPE), "tp", scatter_dimension=0, tiled=True
    ).astype(jnp.float32)
    own_rows = (states.astype(jnp.float32) + change).astype(jnp.bfloat16)
    per_learner = rows_here // n_dev
    learner = place // rows_here
    learner_hits = (learner[:, None] == jnp.arange(n_dev, dtype=jnp.int32)[None, :]).astype(
        jnp.int32
    )
    lane_index = learner * per_learner + running_rank(learner_hits)
    placer = jnp.arange(rows_here, dtype=jnp.int32)[:, None] == lane_index[None, :]
    spot_index = place % rows_here
    packed = jnp.dot(
        placer.astype(jnp.bfloat16), own_rows, preferred_element_type=jnp.float32
    ).astype(jnp.bfloat16)
    packed_spot = jnp.sum(placer.astype(jnp.int32) * spot_index[None, :], axis=1)
    spot_lanes = jnp.where(
        jnp.arange(128, dtype=jnp.int32)[None, :] == 0, packed_spot[:, None], 0
    ).astype(jnp.bfloat16)
    arrivals = lax.all_to_all(
        jnp.concatenate([packed, spot_lanes], axis=1).reshape(n_dev, per_learner, feature_width + 128),
        ("member", "tp"),
        split_axis=0,
        concat_axis=0,
        tiled=True,
    )
    arrivals = arrivals.reshape(n_dev * per_learner, feature_width + 128)
    arrival_spots = arrivals[:, feature_width].astype(jnp.int32)
    settle = (jnp.arange(rows_here, dtype=jnp.int32)[:, None] == arrival_spots[None, :]).astype(
        jnp.bfloat16
    )
    imagined = jnp.dot(
        settle, arrivals[:, :feature_width], preferred_element_type=jnp.float32
    ).astype(jnp.bfloat16)
    policy_normed = rms_scale(imagined.astype(jnp.float32), policy_gain).astype(jnp.bfloat16)
    action = jnp.tanh(jnp.dot(policy_normed, w_policy, preferred_element_type=jnp.float32)).astype(
        jnp.bfloat16
    )
    return (imagined, action)


def solution(mesh):
    in_specs = (
        P(("rep", "member", "tp"), None),
        P(("rep", "member", "tp"), None),
        P(("rep", "member", "tp")),
        P(),
        P("member", None, "tp"),
        P("member", "tp", None),
        P(),
        P(),
    )
    out_specs = (P(("rep", "member", "tp"), None), P(("rep", "member", "tp"), None))
    return jax.shard_map(local, mesh=mesh, in_specs=in_specs, out_specs=out_specs, check_vma=False)
```

```python
import jax
import jax.numpy as jnp
from jax import lax
from jax.sharding import PartitionSpec as P

PARTIAL_DTYPE = jnp.bfloat16


def from_partner(value, axis, distance):
    return lax.ppermute(value, axis, [(i, i ^ 1 << distance) for i in range(lax.axis_size(axis))])


def from_chip_behind(value, axis, chips_back):
    size = lax.axis_size(axis)
    return lax.ppermute(value, axis, [(i, (i + 2 * chips_back) % size) for i in range(size)])


def swap_parts(value):
    n_rep = lax.axis_size("rep")
    return [value] + [
        lax.ppermute(value, "rep", [(i, (i + step) % n_rep) for i in range(n_rep)])
        for step in range(1, n_rep)
    ]


def fetch_shared(up, down, chips_back):
    n_rep = lax.axis_size("rep")
    share = up.shape[1] // n_rep
    rep_here = lax.axis_index("rep")
    got_up = from_chip_behind(
        lax.dynamic_slice_in_dim(up, rep_here * share, share, axis=1), "member", chips_back
    )
    got_up, down = lax.optimization_barrier((got_up, down))
    got_down = from_chip_behind(
        lax.dynamic_slice_in_dim(down, rep_here * share, share, axis=0), "member", chips_back
    )
    up_parts = swap_parts(got_up)
    down_parts = swap_parts(got_down)
    partner_up = [from_partner(part, "member", 0) for part in up_parts]
    partner_down = [from_partner(part, "member", 0) for part in down_parts]
    return (
        jnp.concatenate(up_parts + partner_up, axis=1),
        jnp.concatenate(down_parts + partner_down, axis=0),
    )


def rms_scale(values, gain):
    mean_square = jnp.mean(values * values, axis=-1, keepdims=True)
    return values * lax.rsqrt(mean_square + 1e-06) * gain


def running_rank(member_hits):
    return jnp.sum((jnp.cumsum(member_hits, axis=0) - member_hits) * member_hits, axis=1)


def local(states, member_of, place, norm_gain, w_up, w_down, policy_gain, w_policy):
    n_member = lax.axis_size("member")
    n_tp = lax.axis_size("tp")
    n_dev = n_member * n_tp
    member_total = n_member // 2
    rows_here = states.shape[0]
    feature_width = states.shape[1]
    own_member = lax.axis_index("member") // 2
    own_block = (own_member, w_up[0], w_down[0])
    fetched = [
        (
            (own_member - back + member_total) % member_total,
            *fetch_shared(w_up[0], w_down[0], back),
        )
        for back in range(1, member_total)
    ]
    member = member_of[:, 0]
    gain_rows = jnp.take(norm_gain, member, axis=0)
    normed = rms_scale(states.astype(jnp.float32), gain_rows).astype(jnp.bfloat16)
    member_lanes = jnp.where(
        jnp.arange(128, dtype=jnp.int32)[None, :] == 0, member[:, None], 0
    ).astype(jnp.bfloat16)
    gathered = lax.all_gather(
        jnp.concatenate([normed, member_lanes], axis=1), "tp", axis=0, tiled=True
    )
    gathered_rows = gathered[:, :feature_width]
    gathered_member = gathered[:, feature_width].astype(jnp.int32)

    def apply_block(block_member, up_here, down_here):
        keep = (gathered_member == block_member).astype(jnp.bfloat16)[:, None]
        hidden = jax.nn.gelu(
            jnp.dot(gathered_rows, up_here, preferred_element_type=jnp.float32)
        ).astype(jnp.bfloat16) * keep
        return jnp.dot(hidden, down_here, preferred_element_type=jnp.float32)

    def apply_pair(block_member, up_here, down_here):
        both_up = jnp.concatenate([up_here, from_partner(up_here, "member", 0)], axis=1)
        both_down = jnp.concatenate([down_here, from_partner(down_here, "member", 0)], axis=0)
        return apply_block(block_member, both_up, both_down)

    terms = [apply_pair(*own_block)]
    for block_member, up_here, down_here in fetched:
        terms, up_here, down_here = lax.optimization_barrier((terms, up_here, down_here))
        terms = terms + [apply_block(block_member, up_here, down_here)]
    tp_here = lax.axis_index("tp")
    by_target = [term.reshape(n_tp, rows_here, feature_width) for term in terms]

    def slice_for(target):
        pieces = [lax.dynamic_index_in_dim(term, target, 0, keepdims=False) for term in by_target]
        total = pieces[0]
        for piece in pieces[1:]:
            total = total + piece
        return total

    change = slice_for(tp_here)
    for shift in range(1, n_tp):
        change = change + lax.ppermute(
            slice_for((tp_here + shift) % n_tp).astype(PARTIAL_DTYPE),
            "tp",
            [(i, (i + shift) % n_tp) for i in range(n_tp)],
        ).astype(jnp.float32)
    own_rows = (states.astype(jnp.float32) + change).astype(jnp.bfloat16)
    per_learner = rows_here // n_dev
    learner = place // rows_here
    learner_hits = (learner[:, None] == jnp.arange(n_dev, dtype=jnp.int32)[None, :]).astype(
        jnp.int32
    )
    lane_index = learner * per_learner + running_rank(learner_hits)
    placer = jnp.arange(rows_here, dtype=jnp.int32)[:, None] == lane_index[None, :]
    spot_index = place % rows_here
    packed = jnp.dot(
        placer.astype(jnp.bfloat16), own_rows, preferred_element_type=jnp.float32
    ).astype(jnp.bfloat16)
    packed_spot = jnp.sum(placer.astype(jnp.int32) * spot_index[None, :], axis=1)
    arrival_spots = lax.all_to_all(
        packed_spot.reshape(n_dev, per_learner), ("member", "tp"), split_axis=0, concat_axis=0, tiled=True
    ).reshape(n_dev * per_learner)
    settle = (jnp.arange(rows_here, dtype=jnp.int32)[:, None] == arrival_spots[None, :]).astype(
        jnp.bfloat16
    )
    arrivals = lax.all_to_all(
        packed.reshape(n_dev, per_learner, feature_width),
        ("member", "tp"),
        split_axis=0,
        concat_axis=0,
        tiled=True,
    ).reshape(n_dev * per_learner, feature_width)
    imagined = jnp.dot(settle, arrivals, preferred_element_type=jnp.float32).astype(jnp.bfloat16)
    policy_normed = rms_scale(imagined.astype(jnp.float32), policy_gain).astype(jnp.bfloat16)
    action = jnp.tanh(jnp.dot(policy_normed, w_policy, preferred_element_type=jnp.float32)).astype(
        jnp.bfloat16
    )
    return (imagined, action)


def solution(mesh):
    in_specs = (
        P(("rep", "member", "tp"), None),
        P(("rep", "member", "tp"), None),
        P(("rep", "member", "tp")),
        P(),
        P("member", None, "tp"),
        P("member", "tp", None),
        P(),
        P(),
    )
    out_specs = (P(("rep", "member", "tp"), None), P(("rep", "member", "tp"), None))
    return jax.shard_map(local, mesh=mesh, in_specs=in_specs, out_specs=out_specs, check_vma=False)
```

```python
import jax
import jax.numpy as jnp
from jax import lax
from jax.sharding import PartitionSpec as P

PARTIAL_DTYPE = jnp.bfloat16


def from_partner(value, axis, distance):
    return lax.ppermute(value, axis, [(i, i ^ 1 << distance) for i in range(lax.axis_size(axis))])


def from_chip_behind(value, axis, chips_back):
    size = lax.axis_size(axis)
    return lax.ppermute(value, axis, [(i, (i + 2 * chips_back) % size) for i in range(size)])


def swap_parts(value):
    n_rep = lax.axis_size("rep")
    return [value] + [
        lax.ppermute(value, "rep", [(i, (i + step) % n_rep) for i in range(n_rep)])
        for step in range(1, n_rep)
    ]


def fetch_shared(up, down, chips_back):
    n_rep = lax.axis_size("rep")
    share = up.shape[1] // n_rep
    rep_here = lax.axis_index("rep")
    got_up = from_chip_behind(
        lax.dynamic_slice_in_dim(up, rep_here * share, share, axis=1), "member", chips_back
    )
    got_up, down = lax.optimization_barrier((got_up, down))
    got_down = from_chip_behind(
        lax.dynamic_slice_in_dim(down, rep_here * share, share, axis=0), "member", chips_back
    )
    up_parts = swap_parts(got_up)
    down_parts = swap_parts(got_down)
    partner_up = [from_partner(part, "member", 0) for part in up_parts]
    partner_down = [from_partner(part, "member", 0) for part in down_parts]
    return up_parts + partner_up, down_parts + partner_down


def rms_scale(values, gain):
    mean_square = jnp.mean(values * values, axis=-1, keepdims=True)
    return values * lax.rsqrt(mean_square + 1e-06) * gain


def running_rank(member_hits):
    return jnp.sum((jnp.cumsum(member_hits, axis=0) - member_hits) * member_hits, axis=1)


def local(states, member_of, place, norm_gain, w_up, w_down, policy_gain, w_policy):
    n_member = lax.axis_size("member")
    n_tp = lax.axis_size("tp")
    n_dev = n_member * n_tp
    member_total = n_member // 2
    rows_here = states.shape[0]
    feature_width = states.shape[1]
    own_member = lax.axis_index("member") // 2
    own_block = (own_member, w_up[0], w_down[0])
    fetched = [
        (
            (own_member - back + member_total) % member_total,
            *fetch_shared(w_up[0], w_down[0], back),
        )
        for back in range(1, member_total)
    ]
    member = member_of[:, 0]
    gain_rows = jnp.take(norm_gain, member, axis=0)
    normed = rms_scale(states.astype(jnp.float32), gain_rows).astype(jnp.bfloat16)
    member_lanes = jnp.where(
        jnp.arange(128, dtype=jnp.int32)[None, :] == 0, member[:, None], 0
    ).astype(jnp.bfloat16)
    gathered = lax.all_gather(
        jnp.concatenate([normed, member_lanes], axis=1), "tp", axis=0, tiled=True
    )
    gathered_rows = gathered[:, :feature_width]
    gathered_member = gathered[:, feature_width].astype(jnp.int32)

    def apply_block(block_member, up_here, down_here):
        keep = (gathered_member == block_member).astype(jnp.bfloat16)[:, None]
        hidden = jax.nn.gelu(
            jnp.dot(gathered_rows, up_here, preferred_element_type=jnp.float32)
        ).astype(jnp.bfloat16) * keep
        return jnp.dot(hidden, down_here, preferred_element_type=jnp.float32)

    def apply_pair(block_member, up_here, down_here):
        both_up = jnp.concatenate([up_here, from_partner(up_here, "member", 0)], axis=1)
        both_down = jnp.concatenate([down_here, from_partner(down_here, "member", 0)], axis=0)
        return apply_block(block_member, both_up, both_down)

    terms = [apply_pair(*own_block)]
    for block_member, up_here, down_here in fetched:
        terms, up_here, down_here = lax.optimization_barrier((terms, up_here, down_here))
        terms = terms + [
            apply_block(
                block_member, jnp.concatenate(up_here, axis=1), jnp.concatenate(down_here, axis=0)
            )
        ]
    tp_here = lax.axis_index("tp")
    by_target = [term.reshape(n_tp, rows_here, feature_width) for term in terms]

    def slice_for(target):
        pieces = [lax.dynamic_index_in_dim(term, target, 0, keepdims=False) for term in by_target]
        total = pieces[0]
        for piece in pieces[1:]:
            total = total + piece
        return total

    change = slice_for(tp_here)
    for shift in range(1, n_tp):
        change = change + lax.ppermute(
            slice_for((tp_here + shift) % n_tp).astype(PARTIAL_DTYPE),
            "tp",
            [(i, (i + shift) % n_tp) for i in range(n_tp)],
        ).astype(jnp.float32)
    own_rows = (states.astype(jnp.float32) + change).astype(jnp.bfloat16)
    per_learner = rows_here // n_dev
    learner = place // rows_here
    learner_hits = (learner[:, None] == jnp.arange(n_dev, dtype=jnp.int32)[None, :]).astype(
        jnp.int32
    )
    lane_index = learner * per_learner + running_rank(learner_hits)
    placer = jnp.arange(rows_here, dtype=jnp.int32)[:, None] == lane_index[None, :]
    spot_index = place % rows_here
    packed = jnp.dot(
        placer.astype(jnp.bfloat16), own_rows, preferred_element_type=jnp.float32
    ).astype(jnp.bfloat16)
    packed_spot = jnp.sum(placer.astype(jnp.int32) * spot_index[None, :], axis=1)
    spot_lanes = jnp.where(
        jnp.arange(128, dtype=jnp.int32)[None, :] == 0, packed_spot[:, None], 0
    ).astype(jnp.bfloat16)
    arrivals = lax.all_to_all(
        jnp.concatenate([packed, spot_lanes], axis=1).reshape(n_dev, per_learner, feature_width + 128),
        ("member", "tp"),
        split_axis=0,
        concat_axis=0,
        tiled=True,
    )
    arrivals = arrivals.reshape(n_dev * per_learner, feature_width + 128)
    arrival_spots = arrivals[:, feature_width].astype(jnp.int32)
    settle = (jnp.arange(rows_here, dtype=jnp.int32)[:, None] == arrival_spots[None, :]).astype(
        jnp.bfloat16
    )
    imagined = jnp.dot(
        settle, arrivals[:, :feature_width], preferred_element_type=jnp.float32
    ).astype(jnp.bfloat16)
    policy_normed = rms_scale(imagined.astype(jnp.float32), policy_gain).astype(jnp.bfloat16)
    action = jnp.tanh(jnp.dot(policy_normed, w_policy, preferred_element_type=jnp.float32)).astype(
        jnp.bfloat16
    )
    return (imagined, action)


def solution(mesh):
    in_specs = (
        P(("rep", "member", "tp"), None),
        P(("rep", "member", "tp"), None),
        P(("rep", "member", "tp")),
        P(),
        P("member", None, "tp"),
        P("member", "tp", None),
        P(),
        P(),
    )
    out_specs = (P(("rep", "member", "tp"), None), P(("rep", "member", "tp"), None))
    return jax.shard_map(local, mesh=mesh, in_specs=in_specs, out_specs=out_specs, check_vma=False)
```

```python
import jax
import jax.numpy as jnp
from jax import lax
from jax.sharding import PartitionSpec as P

PARTIAL_DTYPE = jnp.bfloat16


def from_partner(value, axis, distance):
    return lax.ppermute(value, axis, [(i, i ^ 1 << distance) for i in range(lax.axis_size(axis))])


def from_chip_behind(value, axis, chips_back):
    size = lax.axis_size(axis)
    return lax.ppermute(value, axis, [(i, (i + 2 * chips_back) % size) for i in range(size)])


def swap_parts(value):
    n_rep = lax.axis_size("rep")
    return [value] + [
        lax.ppermute(value, "rep", [(i, (i + step) % n_rep) for i in range(n_rep)])
        for step in range(1, n_rep)
    ]


def fetch_shared(up, down, chips_back):
    n_rep = lax.axis_size("rep")
    share = up.shape[1] // n_rep
    rep_here = lax.axis_index("rep")
    got_up = from_chip_behind(
        lax.dynamic_slice_in_dim(up, rep_here * share, share, axis=1), "member", chips_back
    )
    got_up, down = lax.optimization_barrier((got_up, down))
    got_down = from_chip_behind(
        lax.dynamic_slice_in_dim(down, rep_here * share, share, axis=0), "member", chips_back
    )
    up_parts = swap_parts(got_up)
    down_parts = swap_parts(got_down)
    partner_up = [from_partner(part, "member", 0) for part in up_parts]
    partner_down = [from_partner(part, "member", 0) for part in down_parts]
    return up_parts + partner_up, down_parts + partner_down


def rms_scale(values, gain):
    mean_square = jnp.mean(values * values, axis=-1, keepdims=True)
    return values * lax.rsqrt(mean_square + 1e-06) * gain


def running_rank(member_hits):
    return jnp.sum((jnp.cumsum(member_hits, axis=0) - member_hits) * member_hits, axis=1)


def local(states, member_of, place, norm_gain, w_up, w_down, policy_gain, w_policy):
    n_member = lax.axis_size("member")
    n_tp = lax.axis_size("tp")
    n_dev = n_member * n_tp
    member_total = n_member // 2
    rows_here = states.shape[0]
    feature_width = states.shape[1]
    own_member = lax.axis_index("member") // 2
    own_block = (own_member, w_up[0], w_down[0])
    fetched = [
        (
            (own_member - back + member_total) % member_total,
            *fetch_shared(w_up[0], w_down[0], back),
        )
        for back in range(1, member_total)
    ]
    member = member_of[:, 0]
    gain_rows = jnp.take(norm_gain, member, axis=0)
    normed = rms_scale(states.astype(jnp.float32), gain_rows).astype(jnp.bfloat16)
    member_lanes = jnp.where(
        jnp.arange(128, dtype=jnp.int32)[None, :] == 0, member[:, None], 0
    ).astype(jnp.bfloat16)
    to_gather = jnp.concatenate([normed, member_lanes], axis=1)
    if fetched:
        to_gather, _ = lax.optimization_barrier((to_gather, fetched[0][1][0]))
    gathered = lax.all_gather(to_gather, "tp", axis=0, tiled=True)
    gathered_rows = gathered[:, :feature_width]
    gathered_member = gathered[:, feature_width].astype(jnp.int32)

    def apply_block(block_member, up_here, down_here):
        keep = (gathered_member == block_member).astype(jnp.bfloat16)[:, None]
        hidden = jax.nn.gelu(
            jnp.dot(gathered_rows, up_here, preferred_element_type=jnp.float32)
        ).astype(jnp.bfloat16) * keep
        return jnp.dot(hidden, down_here, preferred_element_type=jnp.float32)

    def apply_pair(block_member, up_here, down_here):
        both_up = jnp.concatenate([up_here, from_partner(up_here, "member", 0)], axis=1)
        both_down = jnp.concatenate([down_here, from_partner(down_here, "member", 0)], axis=0)
        return apply_block(block_member, both_up, both_down)

    terms = [apply_pair(*own_block)]
    for block_member, up_here, down_here in fetched:
        terms, up_here, down_here = lax.optimization_barrier((terms, up_here, down_here))
        terms = terms + [
            apply_block(
                block_member, jnp.concatenate(up_here, axis=1), jnp.concatenate(down_here, axis=0)
            )
        ]
    tp_here = lax.axis_index("tp")
    by_target = [term.reshape(n_tp, rows_here, feature_width) for term in terms]

    def slice_for(target):
        pieces = [lax.dynamic_index_in_dim(term, target, 0, keepdims=False) for term in by_target]
        total = pieces[0]
        for piece in pieces[1:]:
            total = total + piece
        return total

    change = slice_for(tp_here)
    for shift in range(1, n_tp):
        change = change + lax.ppermute(
            slice_for((tp_here + shift) % n_tp).astype(PARTIAL_DTYPE),
            "tp",
            [(i, (i + shift) % n_tp) for i in range(n_tp)],
        ).astype(jnp.float32)
    own_rows = (states.astype(jnp.float32) + change).astype(jnp.bfloat16)
    per_learner = rows_here // n_dev
    learner = place // rows_here
    learner_hits = (learner[:, None] == jnp.arange(n_dev, dtype=jnp.int32)[None, :]).astype(
        jnp.int32
    )
    lane_index = learner * per_learner + running_rank(learner_hits)
    placer = jnp.arange(rows_here, dtype=jnp.int32)[:, None] == lane_index[None, :]
    spot_index = place % rows_here
    packed = jnp.dot(
        placer.astype(jnp.bfloat16), own_rows, preferred_element_type=jnp.float32
    ).astype(jnp.bfloat16)
    packed_spot = jnp.sum(placer.astype(jnp.int32) * spot_index[None, :], axis=1)
    spot_lanes = jnp.where(
        jnp.arange(128, dtype=jnp.int32)[None, :] == 0, packed_spot[:, None], 0
    ).astype(jnp.bfloat16)
    arrivals = lax.all_to_all(
        jnp.concatenate([packed, spot_lanes], axis=1).reshape(n_dev, per_learner, feature_width + 128),
        ("member", "tp"),
        split_axis=0,
        concat_axis=0,
        tiled=True,
    )
    arrivals = arrivals.reshape(n_dev * per_learner, feature_width + 128)
    arrival_spots = arrivals[:, feature_width].astype(jnp.int32)
    settle = (jnp.arange(rows_here, dtype=jnp.int32)[:, None] == arrival_spots[None, :]).astype(
        jnp.bfloat16
    )
    imagined = jnp.dot(
        settle, arrivals[:, :feature_width], preferred_element_type=jnp.float32
    ).astype(jnp.bfloat16)
    policy_normed = rms_scale(imagined.astype(jnp.float32), policy_gain).astype(jnp.bfloat16)
    action = jnp.tanh(jnp.dot(policy_normed, w_policy, preferred_element_type=jnp.float32)).astype(
        jnp.bfloat16
    )
    return (imagined, action)


def solution(mesh):
    in_specs = (
        P(("rep", "member", "tp"), None),
        P(("rep", "member", "tp"), None),
        P(("rep", "member", "tp")),
        P(),
        P("member", None, "tp"),
        P("member", "tp", None),
        P(),
        P(),
    )
    out_specs = (P(("rep", "member", "tp"), None), P(("rep", "member", "tp"), None))
    return jax.shard_map(local, mesh=mesh, in_specs=in_specs, out_specs=out_specs, check_vma=False)
```

```python
import jax
import jax.numpy as jnp
from jax import lax
from jax.sharding import PartitionSpec as P

PARTIAL_DTYPE = jnp.bfloat16


def from_partner(value, axis, distance):
    return lax.ppermute(value, axis, [(i, i ^ 1 << distance) for i in range(lax.axis_size(axis))])


def from_chip_behind(value, axis, chips_back):
    size = lax.axis_size(axis)
    return lax.ppermute(value, axis, [(i, (i + 2 * chips_back) % size) for i in range(size)])


def swap_parts(value):
    n_rep = lax.axis_size("rep")
    return [value] + [
        lax.ppermute(value, "rep", [(i, (i + step) % n_rep) for i in range(n_rep)])
        for step in range(1, n_rep)
    ]


def fetch_shared(up, down, chips_back):
    n_rep = lax.axis_size("rep")
    share = up.shape[1] // n_rep
    rep_here = lax.axis_index("rep")
    got_up = from_chip_behind(
        lax.dynamic_slice_in_dim(up, rep_here * share, share, axis=1), "member", chips_back
    )
    got_up, down = lax.optimization_barrier((got_up, down))
    got_down = from_chip_behind(
        lax.dynamic_slice_in_dim(down, rep_here * share, share, axis=0), "member", chips_back
    )
    up_parts = swap_parts(got_up)
    down_parts = swap_parts(got_down)
    partner_up = [from_partner(part, "member", 0) for part in up_parts]
    partner_down = [from_partner(part, "member", 0) for part in down_parts]
    return up_parts + partner_up, down_parts + partner_down


def rms_scale(values, gain):
    mean_square = jnp.mean(values * values, axis=-1, keepdims=True)
    return values * lax.rsqrt(mean_square + 1e-06) * gain


def running_rank(member_hits):
    return jnp.sum((jnp.cumsum(member_hits, axis=0) - member_hits) * member_hits, axis=1)


def local(states, member_of, place, norm_gain, w_up, w_down, policy_gain, w_policy):
    n_member = lax.axis_size("member")
    n_tp = lax.axis_size("tp")
    n_dev = n_member * n_tp
    member_total = n_member // 2
    rows_here = states.shape[0]
    feature_width = states.shape[1]
    own_member = lax.axis_index("member") // 2
    own_block = (own_member, w_up[0], w_down[0])
    fetched = [
        (
            (own_member - back + member_total) % member_total,
            *fetch_shared(w_up[0], w_down[0], back),
        )
        for back in range(1, member_total)
    ]
    per_learner = rows_here // n_dev
    learner = place // rows_here
    learner_hits = (learner[:, None] == jnp.arange(n_dev, dtype=jnp.int32)[None, :]).astype(
        jnp.int32
    )
    lane_index = learner * per_learner + running_rank(learner_hits)
    placer = jnp.arange(rows_here, dtype=jnp.int32)[:, None] == lane_index[None, :]
    states = jnp.dot(
        placer.astype(jnp.bfloat16), states, preferred_element_type=jnp.float32
    ).astype(jnp.bfloat16)
    member = jnp.sum(placer.astype(jnp.int32) * member_of[:, 0][None, :], axis=1)
    packed_spot = jnp.sum(placer.astype(jnp.int32) * (place % rows_here)[None, :], axis=1)
    gain_rows = jnp.take(norm_gain, member, axis=0)
    normed = rms_scale(states.astype(jnp.float32), gain_rows).astype(jnp.bfloat16)
    member_lanes = jnp.where(
        jnp.arange(128, dtype=jnp.int32)[None, :] == 0, member[:, None], 0
    ).astype(jnp.bfloat16)
    gathered = lax.all_gather(
        jnp.concatenate([normed, member_lanes], axis=1), "tp", axis=0, tiled=True
    )
    gathered_rows = gathered[:, :feature_width]
    gathered_member = gathered[:, feature_width].astype(jnp.int32)

    def apply_block(block_member, up_here, down_here):
        keep = (gathered_member == block_member).astype(jnp.bfloat16)[:, None]
        hidden = jax.nn.gelu(
            jnp.dot(gathered_rows, up_here, preferred_element_type=jnp.float32)
        ).astype(jnp.bfloat16) * keep
        return jnp.dot(hidden, down_here, preferred_element_type=jnp.float32)

    def apply_pair(block_member, up_here, down_here):
        both_up = jnp.concatenate([up_here, from_partner(up_here, "member", 0)], axis=1)
        both_down = jnp.concatenate([down_here, from_partner(down_here, "member", 0)], axis=0)
        return apply_block(block_member, both_up, both_down)

    terms = [apply_pair(*own_block)]
    for block_member, up_here, down_here in fetched:
        terms, up_here, down_here = lax.optimization_barrier((terms, up_here, down_here))
        terms = terms + [
            apply_block(
                block_member, jnp.concatenate(up_here, axis=1), jnp.concatenate(down_here, axis=0)
            )
        ]
    tp_here = lax.axis_index("tp")
    by_target = [term.reshape(n_tp, rows_here, feature_width) for term in terms]

    def slice_for(target):
        pieces = [lax.dynamic_index_in_dim(term, target, 0, keepdims=False) for term in by_target]
        total = pieces[0]
        for piece in pieces[1:]:
            total = total + piece
        return total

    change = slice_for(tp_here)
    for shift in range(1, n_tp):
        change = change + lax.ppermute(
            slice_for((tp_here + shift) % n_tp).astype(PARTIAL_DTYPE),
            "tp",
            [(i, (i + shift) % n_tp) for i in range(n_tp)],
        ).astype(jnp.float32)
    packed = (states.astype(jnp.float32) + change).astype(jnp.bfloat16)
    spot_lanes = jnp.where(
        jnp.arange(128, dtype=jnp.int32)[None, :] == 0, packed_spot[:, None], 0
    ).astype(jnp.bfloat16)
    arrivals = lax.all_to_all(
        jnp.concatenate([packed, spot_lanes], axis=1).reshape(n_dev, per_learner, feature_width + 128),
        ("member", "tp"),
        split_axis=0,
        concat_axis=0,
        tiled=True,
    )
    arrivals = arrivals.reshape(n_dev * per_learner, feature_width + 128)
    arrival_spots = arrivals[:, feature_width].astype(jnp.int32)
    settle = (jnp.arange(rows_here, dtype=jnp.int32)[:, None] == arrival_spots[None, :]).astype(
        jnp.bfloat16
    )
    imagined = jnp.dot(
        settle, arrivals[:, :feature_width], preferred_element_type=jnp.float32
    ).astype(jnp.bfloat16)
    policy_normed = rms_scale(imagined.astype(jnp.float32), policy_gain).astype(jnp.bfloat16)
    action = jnp.tanh(jnp.dot(policy_normed, w_policy, preferred_element_type=jnp.float32)).astype(
        jnp.bfloat16
    )
    return (imagined, action)


def solution(mesh):
    in_specs = (
        P(("rep", "member", "tp"), None),
        P(("rep", "member", "tp"), None),
        P(("rep", "member", "tp")),
        P(),
        P("member", None, "tp"),
        P("member", "tp", None),
        P(),
        P(),
    )
    out_specs = (P(("rep", "member", "tp"), None), P(("rep", "member", "tp"), None))
    return jax.shard_map(local, mesh=mesh, in_specs=in_specs, out_specs=out_specs, check_vma=False)
```

```python
import jax
import jax.numpy as jnp
from jax import lax
from jax.sharding import PartitionSpec as P

PARTIAL_DTYPE = jnp.bfloat16


def from_partner(value, axis, distance):
    return lax.ppermute(value, axis, [(i, i ^ 1 << distance) for i in range(lax.axis_size(axis))])


def from_chip_behind(value, axis, chips_back):
    size = lax.axis_size(axis)
    return lax.ppermute(value, axis, [(i, (i + 2 * chips_back) % size) for i in range(size)])


def swap_parts(value):
    n_rep = lax.axis_size("rep")
    return [value] + [
        lax.ppermute(value, "rep", [(i, (i + step) % n_rep) for i in range(n_rep)])
        for step in range(1, n_rep)
    ]


def fetch_shared(up, down, chips_back):
    n_rep = lax.axis_size("rep")
    share = up.shape[1] // n_rep
    rep_here = lax.axis_index("rep")
    got_up = from_chip_behind(
        lax.dynamic_slice_in_dim(up, rep_here * share, share, axis=1), "member", chips_back
    )
    got_up, down = lax.optimization_barrier((got_up, down))
    got_down = from_chip_behind(
        lax.dynamic_slice_in_dim(down, rep_here * share, share, axis=0), "member", chips_back
    )
    up_parts = swap_parts(got_up)
    down_parts = swap_parts(got_down)
    partner_up = [from_partner(part, "member", 0) for part in up_parts]
    partner_down = [from_partner(part, "member", 0) for part in down_parts]
    return up_parts + partner_up, down_parts + partner_down


def rms_scale(values, gain):
    mean_square = jnp.mean(values * values, axis=-1, keepdims=True)
    return values * lax.rsqrt(mean_square + 1e-06) * gain


def running_rank(member_hits):
    return jnp.sum((jnp.cumsum(member_hits, axis=0) - member_hits) * member_hits, axis=1)


def local(states, member_of, place, norm_gain, w_up, w_down, policy_gain, w_policy):
    n_member = lax.axis_size("member")
    n_tp = lax.axis_size("tp")
    n_dev = n_member * n_tp
    member_total = n_member // 2
    rows_here = states.shape[0]
    feature_width = states.shape[1]
    own_member = lax.axis_index("member") // 2
    own_block = (own_member, w_up[0], w_down[0])
    fetched = [
        (
            (own_member - back + member_total) % member_total,
            *fetch_shared(w_up[0], w_down[0], back),
        )
        for back in range(1, member_total)
    ]
    per_learner = rows_here // n_dev
    learner = place // rows_here
    learner_hits = (learner[:, None] == jnp.arange(n_dev, dtype=jnp.int32)[None, :]).astype(
        jnp.int32
    )
    lane_index = learner * per_learner + running_rank(learner_hits)
    placer = jnp.arange(rows_here, dtype=jnp.int32)[:, None] == lane_index[None, :]
    states = jnp.dot(
        placer.astype(jnp.bfloat16), states, preferred_element_type=jnp.float32
    ).astype(jnp.bfloat16)
    member = jnp.sum(placer.astype(jnp.int32) * member_of[:, 0][None, :], axis=1)
    packed_spot = jnp.sum(placer.astype(jnp.int32) * (place % rows_here)[None, :], axis=1)
    arrival_spots = lax.all_to_all(
        packed_spot.reshape(n_dev, per_learner), ("member", "tp"), split_axis=0, concat_axis=0, tiled=True
    ).reshape(n_dev * per_learner)
    gain_rows = jnp.take(norm_gain, member, axis=0)
    normed = rms_scale(states.astype(jnp.float32), gain_rows).astype(jnp.bfloat16)
    member_lanes = jnp.where(
        jnp.arange(128, dtype=jnp.int32)[None, :] == 0, member[:, None], 0
    ).astype(jnp.bfloat16)
    to_gather, arrival_spots = lax.optimization_barrier(
        (jnp.concatenate([normed, member_lanes], axis=1), arrival_spots)
    )
    gathered = lax.all_gather(to_gather, "tp", axis=0, tiled=True)
    gathered_rows = gathered[:, :feature_width]
    gathered_member = gathered[:, feature_width].astype(jnp.int32)

    def apply_block(block_member, up_here, down_here):
        keep = (gathered_member == block_member).astype(jnp.bfloat16)[:, None]
        hidden = jax.nn.gelu(
            jnp.dot(gathered_rows, up_here, preferred_element_type=jnp.float32)
        ).astype(jnp.bfloat16) * keep
        return jnp.dot(hidden, down_here, preferred_element_type=jnp.float32)

    def apply_pair(block_member, up_here, down_here):
        both_up = jnp.concatenate([up_here, from_partner(up_here, "member", 0)], axis=1)
        both_down = jnp.concatenate([down_here, from_partner(down_here, "member", 0)], axis=0)
        return apply_block(block_member, both_up, both_down)

    terms = [apply_pair(*own_block)]
    for block_member, up_here, down_here in fetched:
        terms, up_here, down_here = lax.optimization_barrier((terms, up_here, down_here))
        terms = terms + [
            apply_block(
                block_member, jnp.concatenate(up_here, axis=1), jnp.concatenate(down_here, axis=0)
            )
        ]
    tp_here = lax.axis_index("tp")
    by_target = [term.reshape(n_tp, rows_here, feature_width) for term in terms]

    def slice_for(target):
        pieces = [lax.dynamic_index_in_dim(term, target, 0, keepdims=False) for term in by_target]
        total = pieces[0]
        for piece in pieces[1:]:
            total = total + piece
        return total

    change = slice_for(tp_here)
    for shift in range(1, n_tp):
        change = change + lax.ppermute(
            slice_for((tp_here + shift) % n_tp).astype(PARTIAL_DTYPE),
            "tp",
            [(i, (i + shift) % n_tp) for i in range(n_tp)],
        ).astype(jnp.float32)
    packed = (states.astype(jnp.float32) + change).astype(jnp.bfloat16)
    arrivals = lax.all_to_all(
        packed.reshape(n_dev, per_learner, feature_width),
        ("member", "tp"),
        split_axis=0,
        concat_axis=0,
        tiled=True,
    ).reshape(n_dev * per_learner, feature_width)
    settle = (jnp.arange(rows_here, dtype=jnp.int32)[:, None] == arrival_spots[None, :]).astype(
        jnp.bfloat16
    )
    imagined = jnp.dot(settle, arrivals, preferred_element_type=jnp.float32).astype(jnp.bfloat16)
    policy_normed = rms_scale(imagined.astype(jnp.float32), policy_gain).astype(jnp.bfloat16)
    action = jnp.tanh(jnp.dot(policy_normed, w_policy, preferred_element_type=jnp.float32)).astype(
        jnp.bfloat16
    )
    return (imagined, action)


def solution(mesh):
    in_specs = (
        P(("rep", "member", "tp"), None),
        P(("rep", "member", "tp"), None),
        P(("rep", "member", "tp")),
        P(),
        P("member", None, "tp"),
        P("member", "tp", None),
        P(),
        P(),
    )
    out_specs = (P(("rep", "member", "tp"), None), P(("rep", "member", "tp"), None))
    return jax.shard_map(local, mesh=mesh, in_specs=in_specs, out_specs=out_specs, check_vma=False)
```
